256 devices in a mesh: seq: 64 (over x, z, core), head: 4 (over y).
Axes of the slice: x: 4, y: 4, z: 8, core: 2. Of those that a mesh axis runs over, the one named last changes fastest.
Arguments:
- queries: bfloat16 [65536, 2048], P('seq', 'head'), may hold values from -48 to 48
- keys: bfloat16 [65536, 2048], P('seq', 'head'), may hold values from -48 to 48
- values: bfloat16 [65536, 2048], P('seq', 'head'), may hold values from -6 to 6
- memory_keys: bfloat16 [65536, 2048], P('seq', 'head'), may hold values from -48 to 48
- memory_values: bfloat16 [65536, 2048], P('seq', 'head'), may hold values from -6 to 6
- block_ids: int32 [512, 4], P('seq'), may hold values from 0 to 1023, as said below
- gate_bias: float32 [16], P('head'), may hold values from -2 to 2
- out_weight: bfloat16 [2048, 2048], P('head'), may hold values from -0.5 to 0.5
Outputs:
- layer_out: bfloat16 [65536, 2048], P(('seq', 'head'))
The draws below stay inside these ranges and needn't reach their ends.
Inputs may be any that keep to these rules, and one draw needn't show every extreme that they name: `block_ids`: block b belongs to owner b // 16. Among the 8 x 4 ids of one device's rows no id repeats; exactly 2 of them name blocks of owner 64 - 1, block 1023 always among them, and no other owner is named more than 1 times.
All inputs are finite; a program needn't handle non-finite values.
Results may differ from the reference program's by a relative error of at most 0.013.
Values may be sent and summed in bfloat16 or wider, within the bound.
No kernel may reach another device: no remote copies, remote signals or barrier semaphores. Data moves between devices by JAX's collectives and lax.ppermute only.
A program may use at most 192 MiB of HBM per device.

```python
import math
import jax
import jax.numpy as jnp
from jax import lax

D = 2048
HEADS = 16
HDIM = 128
WINDOW = 1024
QBLK = 128
MROWS = 64
TOPM = 4
MEMB_DEV = 16
TOKENS = 65536
QB_DEV = 8
QBLOCKS = 512
MBLOCKS = 1024
N_SEQ = 64
N_HEAD = 4


def request_ids(key):
    per_device = QB_DEV * TOPM
    per_owner = (per_device + N_SEQ) // (N_SEQ + 1)
    hot_count = 2 * per_owner

    def one_device(device_key):
        key_one, key_two, key_three, key_four = jax.random.split(device_key, 4)
        offset_shift = jax.random.randint(key_one, (), 0, MEMB_DEV - hot_count + 1)
        hot_slots = jnp.arange(hot_count, dtype=jnp.int32)
        hot_offsets = jnp.where(hot_slots == 0, MEMB_DEV - 1, MEMB_DEV - 1 - hot_slots - offset_shift)
        hot_ids = (N_SEQ - 1) * MEMB_DEV + hot_offsets
        picks = jax.random.permutation(key_two, (N_SEQ - 1) * per_owner)[:per_device - hot_count]
        owner_index = picks // per_owner
        starts = jax.random.randint(key_three, (N_SEQ - 1,), 0, MEMB_DEV)
        cold_ids = owner_index * MEMB_DEV + (starts[owner_index] + picks % per_owner) % MEMB_DEV
        every_id = jnp.concatenate([hot_ids, cold_ids]).astype(jnp.int32)
        return every_id[jax.random.permutation(key_four, per_device)]
    device_keys = jax.random.split(key, N_SEQ)
    return jax.vmap(one_device)(device_keys).reshape(QBLOCKS, TOPM).astype(jnp.int32)


def drawn_fields(key):
    query_field = 2.0 * jax.random.normal(jax.random.fold_in(key, 21), (TOKENS, D), jnp.float32)
    key_field = jax.random.normal(jax.random.fold_in(key, 22), (TOKENS, D), jnp.float32)
    memory_field = jax.random.normal(jax.random.fold_in(key, 23), (MBLOCKS * MROWS, D), jnp.float32)
    return (query_field, key_field, memory_field)


def draw_queries(key, part):
    return drawn_fields(key)[0].astype(jnp.bfloat16)


def draw_keys(key, part):
    return drawn_fields(key)[1].astype(jnp.bfloat16)


def draw_memory_keys(key, part):
    return drawn_fields(key)[2].astype(jnp.bfloat16)


def draw_block_ids(key, part):
    return request_ids(jax.random.fold_in(key, 7))


def block_scale(own_key, extent, cuts, low, high):
    loudness = 1.0
    for position, parts in cuts:
        heights = jax.random.uniform(jax.random.fold_in(jax.random.fold_in(own_key, 6), position), (parts,), jnp.float32, low / len(cuts), high / len(cuts))
        loudness = loudness * jnp.repeat(jnp.exp(heights), extent[position] // parts).reshape((-1,) + (1,) * (len(extent) - 1 - position))
    return loudness


def normal_values(stream_key, extent, width, reach, shards=(), kind=jnp.bfloat16):
    entries = jax.random.normal(stream_key, extent, jnp.float32) * width
    if len(shards) > 0:
        entries = block_scale(stream_key, extent, shards, -0.22, 0.18) * entries
    return jnp.clip(entries, min=-reach, max=reach).astype(kind)


def setup_inputs(seed: int = 0) -> dict:
    arg_keys = jax.random.split(jax.random.key(seed), 9)
    queries = draw_queries(jax.random.fold_in(arg_keys[8], 71), 0)
    keys = draw_keys(jax.random.fold_in(arg_keys[8], 71), 0)
    values = normal_values(arg_keys[2], (TOKENS, D), 1.0, 6.0, ((0, 64), (1, 4)))
    memory_keys = draw_memory_keys(jax.random.fold_in(arg_keys[8], 71), 0)
    memory_values = normal_values(arg_keys[4], (MBLOCKS * MROWS, D), 1.0, 6.0, ((0, 64), (1, 4)))
    block_ids = draw_block_ids(jax.random.fold_in(arg_keys[8], 71), 0)
    gate_bias = jnp.clip(jax.random.uniform(arg_keys[6], (HEADS,), jnp.float32, -2.0, 2.0) * block_scale(arg_keys[6], (HEADS,), ((0, 4),), -0.4, 0.0), -2.0, 2.0)
    out_weight = normal_values(arg_keys[7], (D, D), (D // 16) ** -0.5, 0.5, ((0, 4),))
    return dict(queries=queries, keys=keys, values=values, memory_keys=memory_keys, memory_values=memory_values, block_ids=block_ids, gate_bias=gate_bias, out_weight=out_weight)


NEG_FILL = -1e+30

def masked_softmax(scores, allowed):
    row_max = lax.optimization_barrier(jnp.max(jnp.where(allowed, scores, NEG_FILL), axis=-1, keepdims=True))
    weights = jnp.where(allowed, jnp.exp(scores - row_max), 0.0)
    return (weights / lax.optimization_barrier(jnp.sum(weights, axis=-1, keepdims=True))).astype(jnp.bfloat16)

def window_part(queries, keys, values):
    tile_rows = math.gcd(TOKENS, 512)
    key_span = tile_rows + WINDOW
    score_scale = 1.0 / math.sqrt(HDIM)
    padded_keys = jnp.concatenate([jnp.zeros((WINDOW, D), keys.dtype), keys])
    padded_values = jnp.concatenate([jnp.zeros((WINDOW, D), values.dtype), values])

    def per_tile(step_index):
        row_start = step_index * tile_rows
        query_tile = lax.dynamic_slice_in_dim(queries, row_start, tile_rows, 0).astype(jnp.float32).reshape(tile_rows, HEADS, HDIM)
        key_tile = lax.dynamic_slice_in_dim(padded_keys, row_start, key_span, 0).astype(jnp.float32).reshape(key_span, HEADS, HDIM)
        value_tile = lax.dynamic_slice_in_dim(padded_values, row_start, key_span, 0).astype(jnp.float32).reshape(key_span, HEADS, HDIM)
        scores = jnp.einsum('qhd,khd->hqk', query_tile, key_tile) * score_scale
        query_pos = row_start + jnp.arange(tile_rows, dtype=jnp.int32)
        key_pos = row_start - WINDOW + jnp.arange(key_span, dtype=jnp.int32)
        allowed = (key_pos[None, :] <= query_pos[:, None]) & (key_pos[None, :] > query_pos[:, None] - WINDOW) & (key_pos[None, :] >= 0)
        weights = masked_softmax(scores, allowed[None]).astype(jnp.float32)
        return jnp.einsum('hqk,khd->qhd', weights, value_tile)
    return lax.map(per_tile, jnp.arange(TOKENS // tile_rows, dtype=jnp.int32)).reshape(TOKENS, HEADS, HDIM)

def memory_part(queries, memory_keys, memory_values, block_ids):
    score_scale = 1.0 / math.sqrt(HDIM)
    key_blocks = memory_keys.reshape(MBLOCKS, MROWS, D)
    value_blocks = memory_values.reshape(MBLOCKS, MROWS, D)

    def per_block(block_index):
        query_tile = lax.dynamic_slice_in_dim(queries, block_index * QBLK, QBLK, 0).astype(jnp.float32).reshape(QBLK, HEADS, HDIM)
        chosen = block_ids[block_index]
        key_tile = key_blocks[chosen].astype(jnp.float32).reshape(TOPM * MROWS, HEADS, HDIM)
        value_tile = value_blocks[chosen].astype(jnp.float32).reshape(TOPM * MROWS, HEADS, HDIM)
        scores = jnp.einsum('qhd,khd->hqk', query_tile, key_tile) * score_scale
        weights = masked_softmax(scores, jnp.ones(scores.shape, dtype=bool)).astype(jnp.float32)
        return jnp.einsum('hqk,khd->qhd', weights, value_tile)
    return lax.map(per_block, jnp.arange(QBLOCKS, dtype=jnp.int32)).reshape(TOKENS, HEADS, HDIM)

def reference(queries, keys, values, memory_keys, memory_values, block_ids, gate_bias, out_weight):
    local_part = window_part(queries, keys, values)
    remote = memory_part(queries, memory_keys, memory_values, block_ids)
    mixing = jax.nn.sigmoid(gate_bias)[None, :, None]
    attended = (mixing * remote + (1.0 - mixing) * local_part).reshape(TOKENS, D).astype(jnp.bfloat16)
    group_width = D // N_HEAD
    tile_rows = math.gcd(TOKENS, 4096)

    def per_rows(step_index):
        row_block = lax.dynamic_slice_in_dim(attended, step_index * tile_rows, tile_rows, 0)
        summed = jnp.zeros((tile_rows, D), jnp.float32)
        for head_group in range(N_HEAD):
            lower = head_group * group_width
            partial_term = jnp.dot(row_block[:, lower:lower + group_width], out_weight[lower:lower + group_width], preferred_element_type=jnp.float32).astype(jnp.bfloat16)
            summed = summed + lax.optimization_barrier(partial_term).astype(jnp.float32)
        return summed.astype(jnp.bfloat16)
    return lax.map(per_rows, jnp.arange(TOKENS // tile_rows, dtype=jnp.int32)).reshape(TOKENS, D)
```

```python
import math

import jax
import jax.numpy as jnp
from jax import lax
from jax.sharding import PartitionSpec as P

HDIM = 128
WINDOW = 1024
QBLK = 128
MROWS = 64
TOPM = 4


NEG_FILL = -1e30


def passed_along(value, axis, steps):
    count = lax.axis_size(axis)
    leading, last = (max(0, -steps), min(count, count - steps))
    return lax.ppermute(value, axis, [(source, source + steps) for source in range(leading, last)])


def masked_softmax(scores, allowed):
    row_max = jnp.max(jnp.where(allowed, scores, NEG_FILL), axis=-1, keepdims=True)
    weights = jnp.where(allowed, jnp.exp(scores - row_max), 0.0)
    return (weights / jnp.sum(weights, axis=-1, keepdims=True)).astype(jnp.bfloat16)


def window_attention(queries, ext_keys, ext_values, first_row):
    tok_rows, features = queries.shape
    heads_here = features // HDIM
    tile_rows = math.gcd(tok_rows, 512)
    key_span = tile_rows + WINDOW
    score_scale = 1.0 / math.sqrt(HDIM)

    def per_tile(step_index):
        row_start = step_index * tile_rows
        query_tile = lax.dynamic_slice_in_dim(queries, row_start, tile_rows, 0).reshape(
            tile_rows, heads_here, HDIM
        )
        key_tile = lax.dynamic_slice_in_dim(ext_keys, row_start, key_span, 0).reshape(
            key_span, heads_here, HDIM
        )
        value_tile = lax.dynamic_slice_in_dim(ext_values, row_start, key_span, 0).reshape(
            key_span, heads_here, HDIM
        )
        scores = (
            jnp.einsum("qhd,khd->hqk", query_tile, key_tile, preferred_element_type=jnp.float32)
            * score_scale
        )
        query_pos = first_row + row_start + jnp.arange(tile_rows, dtype=jnp.int32)
        key_pos = first_row + row_start - WINDOW + jnp.arange(key_span, dtype=jnp.int32)
        allowed = (
            (key_pos[None, :] <= query_pos[:, None])
            & (key_pos[None, :] > query_pos[:, None] - WINDOW)
            & (key_pos[None, :] >= 0)
        )
        attend_weights = masked_softmax(scores, allowed[None])
        return jnp.einsum(
            "hqk,khd->qhd", attend_weights, value_tile, preferred_element_type=jnp.float32
        )

    return lax.map(per_tile, jnp.arange(tok_rows // tile_rows, dtype=jnp.int32)).reshape(
        tok_rows, heads_here, HDIM
    )


def memory_attention(queries, fetched):
    tok_rows, features = queries.shape
    heads_here = features // HDIM
    block_count = tok_rows // QBLK
    score_scale = 1.0 / math.sqrt(HDIM)
    query_blocks = queries.reshape(block_count, QBLK, heads_here, HDIM)
    key_blocks = fetched[:, 0].reshape(block_count, TOPM * MROWS, heads_here, HDIM)
    value_blocks = fetched[:, 1].reshape(block_count, TOPM * MROWS, heads_here, HDIM)
    scores = (
        jnp.einsum("bqhd,bkhd->bhqk", query_blocks, key_blocks, preferred_element_type=jnp.float32)
        * score_scale
    )
    attend_weights = masked_softmax(scores, jnp.ones(scores.shape, dtype=bool))
    remote = jnp.einsum(
        "bhqk,bkhd->bqhd", attend_weights, value_blocks, preferred_element_type=jnp.float32
    )
    return remote.reshape(tok_rows, heads_here, HDIM)


def build_table(slot_index, offset, in_use, total_slots):
    matches = (jnp.arange(total_slots, dtype=jnp.int32)[:, None] == slot_index[None, :]) & in_use[
        None, :
    ]
    return jnp.sum(jnp.where(matches, offset[None, :] + 1, 0), axis=1) - 1


def on_device(queries, keys, values, memory_keys, memory_values, block_ids, gate_bias, out_weight):
    tok_rows, features = queries.shape
    owners = lax.axis_size("seq")
    groups = lax.axis_size("head")
    seq_index = lax.axis_index("seq")
    first_row = seq_index * tok_rows
    full_weight = lax.all_gather(out_weight, "head", axis=0, tiled=True)
    request_count = block_ids.shape[0] * block_ids.shape[1]
    wanted = block_ids.reshape(request_count)
    mem_dev = memory_keys.shape[0] // MROWS
    last_block = owners * mem_dev - 1
    owner_index = wanted // mem_dev
    offset = wanted % mem_dev
    is_last = wanted == last_block
    memory_store = jnp.stack(
        (
            memory_keys.reshape(mem_dev, MROWS, features),
            memory_values.reshape(mem_dev, MROWS, features),
        ),
        axis=1,
    )
    slot_table = build_table(owner_index, offset, jnp.logical_not(is_last), owners).reshape(owners, 1)
    asked_for = lax.all_to_all(slot_table, "seq", split_axis=0, concat_axis=0, tiled=True)
    returned = lax.all_to_all(
        memory_store[jnp.maximum(asked_for[:, 0], 0)], "seq", split_axis=0, concat_axis=0, tiled=True
    )
    shared = lax.psum(
        jnp.where(seq_index == owners - 1, memory_store[mem_dev - 1], jnp.zeros_like(memory_store[0])),
        "seq",
    )
    edge_rows = jnp.stack((keys, values))
    before = passed_along(edge_rows, "seq", 1)
    local_part = window_attention(
        queries, jnp.concatenate([before[0], keys]), jnp.concatenate([before[1], values]), first_row
    )
    pool = jnp.concatenate([returned, shared[None]])
    fetched = pool[jnp.where(is_last, owners, owner_index)]
    remote = memory_attention(queries, fetched)
    mixing = jax.nn.sigmoid(gate_bias)[None, :, None]
    attended = (
        (mixing * remote + (1.0 - mixing) * local_part)
        .reshape(tok_rows, features)
        .astype(jnp.bfloat16)
    )
    out_rows = tok_rows // groups
    gathered = lax.all_to_all(
        attended.reshape(groups, out_rows, features), "head", split_axis=0, concat_axis=0, tiled=True
    )
    partials = jnp.einsum(
        "gqf,gfn->gqn",
        gathered,
        full_weight.reshape(groups, features, full_weight.shape[1]),
        preferred_element_type=jnp.float32,
    ).astype(jnp.bfloat16)
    return jnp.sum(partials.astype(jnp.float32), axis=0).astype(jnp.bfloat16)


def solution(mesh):
    in_specs = (
        P("seq", "head"),
        P("seq", "head"),
        P("seq", "head"),
        P("seq", "head"),
        P("seq", "head"),
        P("seq", None),
        P("head"),
        P("head", None),
    )
    out_specs = P(("seq", "head"), None)
    return jax.shard_map(
        on_device, mesh=mesh, in_specs=in_specs, out_specs=out_specs, check_vma=False
    )
```

```python
import math

import jax
import jax.numpy as jnp
from jax import lax
from jax.sharding import PartitionSpec as P

HDIM = 128
WINDOW = 1024
QBLK = 128
MROWS = 64
TOPM = 4


NEG_FILL = -1e30


def passed_along(value, axis, steps):
    count = lax.axis_size(axis)
    leading, last = (max(0, -steps), min(count, count - steps))
    return lax.ppermute(value, axis, [(source, source + steps) for source in range(leading, last)])


def masked_softmax(scores, allowed):
    row_max = jnp.max(jnp.where(allowed, scores, NEG_FILL), axis=-1, keepdims=True)
    weights = jnp.where(allowed, jnp.exp(scores - row_max), 0.0)
    return (weights / jnp.sum(weights, axis=-1, keepdims=True)).astype(jnp.bfloat16)


def window_attention(queries, ext_keys, ext_values, first_row):
    tok_rows, features = queries.shape
    heads_here = features // HDIM
    tile_rows = math.gcd(tok_rows, 512)
    key_span = tile_rows + WINDOW
    score_scale = 1.0 / math.sqrt(HDIM)

    def per_tile(step_index):
        row_start = step_index * tile_rows
        query_tile = lax.dynamic_slice_in_dim(queries, row_start, tile_rows, 0).reshape(
            tile_rows, heads_here, HDIM
        )
        key_tile = lax.dynamic_slice_in_dim(ext_keys, row_start, key_span, 0).reshape(
            key_span, heads_here, HDIM
        )
        value_tile = lax.dynamic_slice_in_dim(ext_values, row_start, key_span, 0).reshape(
            key_span, heads_here, HDIM
        )
        scores = (
            jnp.einsum("qhd,khd->hqk", query_tile, key_tile, preferred_element_type=jnp.float32)
            * score_scale
        )
        query_pos = first_row + row_start + jnp.arange(tile_rows, dtype=jnp.int32)
        key_pos = first_row + row_start - WINDOW + jnp.arange(key_span, dtype=jnp.int32)
        allowed = (
            (key_pos[None, :] <= query_pos[:, None])
            & (key_pos[None, :] > query_pos[:, None] - WINDOW)
            & (key_pos[None, :] >= 0)
        )
        attend_weights = masked_softmax(scores, allowed[None])
        return jnp.einsum(
            "hqk,khd->qhd", attend_weights, value_tile, preferred_element_type=jnp.float32
        )

    return lax.map(per_tile, jnp.arange(tok_rows // tile_rows, dtype=jnp.int32)).reshape(
        tok_rows, heads_here, HDIM
    )


def memory_attention(queries, fetched):
    tok_rows, features = queries.shape
    heads_here = features // HDIM
    block_count = tok_rows // QBLK
    score_scale = 1.0 / math.sqrt(HDIM)
    query_blocks = queries.reshape(block_count, QBLK, heads_here, HDIM)
    key_blocks = fetched[:, 0].reshape(block_count, TOPM * MROWS, heads_here, HDIM)
    value_blocks = fetched[:, 1].reshape(block_count, TOPM * MROWS, heads_here, HDIM)
    scores = (
        jnp.einsum("bqhd,bkhd->bhqk", query_blocks, key_blocks, preferred_element_type=jnp.float32)
        * score_scale
    )
    attend_weights = masked_softmax(scores, jnp.ones(scores.shape, dtype=bool))
    remote = jnp.einsum(
        "bhqk,bkhd->bqhd", attend_weights, value_blocks, preferred_element_type=jnp.float32
    )
    return remote.reshape(tok_rows, heads_here, HDIM)


def build_table(slot_index, offset, in_use, total_slots):
    matches = (jnp.arange(total_slots, dtype=jnp.int32)[:, None] == slot_index[None, :]) & in_use[
        None, :
    ]
    return jnp.sum(jnp.where(matches, offset[None, :] + 1, 0), axis=1) - 1


def on_device(queries, keys, values, memory_keys, memory_values, block_ids, gate_bias, out_weight):
    tok_rows, features = queries.shape
    owners = lax.axis_size("seq")
    groups = lax.axis_size("head")
    seq_index = lax.axis_index("seq")
    first_row = seq_index * tok_rows
    full_weight = lax.all_gather(out_weight, "head", axis=0, tiled=True)
    request_count = block_ids.shape[0] * block_ids.shape[1]
    wanted = block_ids.reshape(request_count)
    mem_dev = memory_keys.shape[0] // MROWS
    last_block = owners * mem_dev - 1
    owner_index = wanted // mem_dev
    offset = wanted % mem_dev
    is_last = wanted == last_block
    memory_store = jnp.stack(
        (
            memory_keys.reshape(mem_dev, MROWS, features),
            memory_values.reshape(mem_dev, MROWS, features),
        ),
        axis=1,
    )
    slot_table = build_table(owner_index, offset, jnp.logical_not(is_last), owners).reshape(owners, 1)
    edge_rows = jnp.stack((keys, values))
    before = passed_along(edge_rows, "seq", 1)
    asked_for = lax.all_to_all(slot_table, "seq", split_axis=0, concat_axis=0, tiled=True)
    outgoing = memory_store[jnp.maximum(asked_for[:, 0], 0)]
    before, outgoing = lax.optimization_barrier((before, outgoing))
    returned = lax.all_to_all(outgoing, "seq", split_axis=0, concat_axis=0, tiled=True)
    shared = lax.psum(
        jnp.where(seq_index == owners - 1, memory_store[mem_dev - 1], jnp.zeros_like(memory_store[0])),
        "seq",
    )
    local_part = window_attention(
        queries, jnp.concatenate([before[0], keys]), jnp.concatenate([before[1], values]), first_row
    )
    fetched = jnp.where(is_last[:, None, None, None], shared[None], returned[owner_index])
    remote = memory_attention(queries, fetched)
    mixing = jax.nn.sigmoid(gate_bias)[None, :, None]
    attended = (
        (mixing * remote + (1.0 - mixing) * local_part)
        .reshape(tok_rows, features)
        .astype(jnp.bfloat16)
    )
    out_rows = tok_rows // groups
    gathered = lax.all_to_all(
        attended.reshape(groups, out_rows, features), "head", split_axis=0, concat_axis=0, tiled=True
    )
    partials = jnp.einsum(
        "gqf,gfn->gqn",
        gathered,
        full_weight.reshape(groups, features, full_weight.shape[1]),
        preferred_element_type=jnp.float32,
    ).astype(jnp.bfloat16)
    return jnp.sum(partials.astype(jnp.float32), axis=0).astype(jnp.bfloat16)


def solution(mesh):
    in_specs = (
        P("seq", "head"),
        P("seq", "head"),
        P("seq", "head"),
        P("seq", "head"),
        P("seq", "head"),
        P("seq", None),
        P("head"),
        P("head", None),
    )
    out_specs = P(("seq", "head"), None)
    return jax.shard_map(
        on_device, mesh=mesh, in_specs=in_specs, out_specs=out_specs, check_vma=False
    )
```

```python
import math

import jax
import jax.numpy as jnp
from jax import lax
from jax.sharding import PartitionSpec as P

HDIM = 128
WINDOW = 1024
QBLK = 128
MROWS = 64
TOPM = 4


NEG_FILL = -1e30


def passed_along(value, axis, steps):
    count = lax.axis_size(axis)
    leading, last = (max(0, -steps), min(count, count - steps))
    return lax.ppermute(value, axis, [(source, source + steps) for source in range(leading, last)])


def masked_softmax(scores, allowed):
    row_max = jnp.max(jnp.where(allowed, scores, NEG_FILL), axis=-1, keepdims=True)
    weights = jnp.where(allowed, jnp.exp(scores - row_max), 0.0)
    return (weights / jnp.sum(weights, axis=-1, keepdims=True)).astype(jnp.bfloat16)


def window_attention(queries, ext_keys, ext_values, first_row):
    tok_rows, features = queries.shape
    heads_here = features // HDIM
    tile_rows = math.gcd(tok_rows, 512)
    key_span = tile_rows + WINDOW
    score_scale = 1.0 / math.sqrt(HDIM)

    def per_tile(step_index):
        row_start = step_index * tile_rows
        query_tile = lax.dynamic_slice_in_dim(queries, row_start, tile_rows, 0).reshape(
            tile_rows, heads_here, HDIM
        )
        key_tile = lax.dynamic_slice_in_dim(ext_keys, row_start, key_span, 0).reshape(
            key_span, heads_here, HDIM
        )
        value_tile = lax.dynamic_slice_in_dim(ext_values, row_start, key_span, 0).reshape(
            key_span, heads_here, HDIM
        )
        scores = (
            jnp.einsum("qhd,khd->hqk", query_tile, key_tile, preferred_element_type=jnp.float32)
            * score_scale
        )
        query_pos = first_row + row_start + jnp.arange(tile_rows, dtype=jnp.int32)
        key_pos = first_row + row_start - WINDOW + jnp.arange(key_span, dtype=jnp.int32)
        allowed = (
            (key_pos[None, :] <= query_pos[:, None])
            & (key_pos[None, :] > query_pos[:, None] - WINDOW)
            & (key_pos[None, :] >= 0)
        )
        attend_weights = masked_softmax(scores, allowed[None])
        return jnp.einsum(
            "hqk,khd->qhd", attend_weights, value_tile, preferred_element_type=jnp.float32
        )

    return lax.map(per_tile, jnp.arange(tok_rows // tile_rows, dtype=jnp.int32)).reshape(
        tok_rows, heads_here, HDIM
    )


def memory_attention(queries, fetched):
    tok_rows, features = queries.shape
    heads_here = features // HDIM
    block_count = tok_rows // QBLK
    score_scale = 1.0 / math.sqrt(HDIM)
    query_blocks = queries.reshape(block_count, QBLK, heads_here, HDIM)
    key_blocks = fetched[:, 0].reshape(block_count, TOPM * MROWS, heads_here, HDIM)
    value_blocks = fetched[:, 1].reshape(block_count, TOPM * MROWS, heads_here, HDIM)
    scores = (
        jnp.einsum("bqhd,bkhd->bhqk", query_blocks, key_blocks, preferred_element_type=jnp.float32)
        * score_scale
    )
    attend_weights = masked_softmax(scores, jnp.ones(scores.shape, dtype=bool))
    remote = jnp.einsum(
        "bhqk,bkhd->bqhd", attend_weights, value_blocks, preferred_element_type=jnp.float32
    )
    return remote.reshape(tok_rows, heads_here, HDIM)


def build_table(slot_index, offset, in_use, total_slots):
    matches = (jnp.arange(total_slots, dtype=jnp.int32)[:, None] == slot_index[None, :]) & in_use[
        None, :
    ]
    return jnp.sum(jnp.where(matches, offset[None, :] + 1, 0), axis=1) - 1


def on_device(queries, keys, values, memory_keys, memory_values, block_ids, gate_bias, out_weight):
    tok_rows, features = queries.shape
    owners = lax.axis_size("seq")
    groups = lax.axis_size("head")
    seq_index = lax.axis_index("seq")
    first_row = seq_index * tok_rows
    full_weight = lax.all_gather(out_weight, "head", axis=0, tiled=True)
    request_count = block_ids.shape[0] * block_ids.shape[1]
    wanted = block_ids.reshape(request_count)
    mem_dev = memory_keys.shape[0] // MROWS
    last_block = owners * mem_dev - 1
    owner_index = wanted // mem_dev
    offset = wanted % mem_dev
    is_last = wanted == last_block
    memory_store = jnp.stack(
        (
            memory_keys.reshape(mem_dev, MROWS, features),
            memory_values.reshape(mem_dev, MROWS, features),
        ),
        axis=1,
    )
    edge_rows = jnp.stack((keys, values))
    before = passed_along(edge_rows, "seq", 1)
    shared = lax.psum(
        jnp.where(seq_index == owners - 1, memory_store[mem_dev - 1], jnp.zeros_like(memory_store[0])),
        "seq",
    )
    every_id = lax.all_gather(block_ids, "seq", axis=0, tiled=True).reshape(owners, request_count)
    mine = (every_id // mem_dev == seq_index) & (every_id != last_block)
    asked_for = jnp.sum(jnp.where(mine, every_id % mem_dev + 1, 0), axis=1) - 1
    outgoing = memory_store[jnp.maximum(asked_for, 0)]
    before, outgoing, shared = lax.optimization_barrier((before, outgoing, shared))
    returned = lax.all_to_all(outgoing, "seq", split_axis=0, concat_axis=0, tiled=True)
    local_part = window_attention(
        queries, jnp.concatenate([before[0], keys]), jnp.concatenate([before[1], values]), first_row
    )
    fetched = jnp.where(is_last[:, None, None, None], shared[None], returned[owner_index])
    remote = memory_attention(queries, fetched)
    mixing = jax.nn.sigmoid(gate_bias)[None, :, None]
    attended = (
        (mixing * remote + (1.0 - mixing) * local_part)
        .reshape(tok_rows, features)
        .astype(jnp.bfloat16)
    )
    out_rows = tok_rows // groups
    gathered = lax.all_to_all(
        attended.reshape(groups, out_rows, features), "head", split_axis=0, concat_axis=0, tiled=True
    )
    partials = jnp.einsum(
        "gqf,gfn->gqn",
        gathered,
        full_weight.reshape(groups, features, full_weight.shape[1]),
        preferred_element_type=jnp.float32,
    ).astype(jnp.bfloat16)
    return jnp.sum(partials.astype(jnp.float32), axis=0).astype(jnp.bfloat16)


def solution(mesh):
    in_specs = (
        P("seq", "head"),
        P("seq", "head"),
        P("seq", "head"),
        P("seq", "head"),
        P("seq", "head"),
        P("seq", None),
        P("head"),
        P("head", None),
    )
    out_specs = P(("seq", "head"), None)
    return jax.shard_map(
        on_device, mesh=mesh, in_specs=in_specs, out_specs=out_specs, check_vma=False
    )
```

```python
import math

import jax
import jax.numpy as jnp
from jax import lax
from jax.experimental import pallas as pl
from jax.experimental.pallas import tpu as pltpu
from jax.sharding import PartitionSpec as P

HDIM = 128
WINDOW = 1024
QBLK = 128
MROWS = 64
TOPM = 4


NEG_FILL = -1e30


def passed_along(value, axis, steps):
    count = lax.axis_size(axis)
    leading, last = (max(0, -steps), min(count, count - steps))
    return lax.ppermute(value, axis, [(source, source + steps) for source in range(leading, last)])


def masked_softmax(scores, allowed):
    row_max = jnp.max(jnp.where(allowed, scores, NEG_FILL), axis=-1, keepdims=True)
    weights = jnp.where(allowed, jnp.exp(scores - row_max), 0.0)
    return (weights / jnp.sum(weights, axis=-1, keepdims=True)).astype(jnp.bfloat16)


def window_attention(queries, ext_keys, ext_values, first_row):
    tok_rows, features = queries.shape
    heads_here = features // HDIM
    tile_rows = math.gcd(tok_rows, 512)
    key_span = tile_rows + WINDOW
    score_scale = 1.0 / math.sqrt(HDIM)

    def per_tile(step_index):
        row_start = step_index * tile_rows
        query_tile = lax.dynamic_slice_in_dim(queries, row_start, tile_rows, 0).reshape(
            tile_rows, heads_here, HDIM
        )
        key_tile = lax.dynamic_slice_in_dim(ext_keys, row_start, key_span, 0).reshape(
            key_span, heads_here, HDIM
        )
        value_tile = lax.dynamic_slice_in_dim(ext_values, row_start, key_span, 0).reshape(
            key_span, heads_here, HDIM
        )
        scores = (
            jnp.einsum("qhd,khd->hqk", query_tile, key_tile, preferred_element_type=jnp.float32)
            * score_scale
        )
        query_pos = first_row + row_start + jnp.arange(tile_rows, dtype=jnp.int32)
        key_pos = first_row + row_start - WINDOW + jnp.arange(key_span, dtype=jnp.int32)
        allowed = (
            (key_pos[None, :] <= query_pos[:, None])
            & (key_pos[None, :] > query_pos[:, None] - WINDOW)
            & (key_pos[None, :] >= 0)
        )
        attend_weights = masked_softmax(scores, allowed[None])
        return jnp.einsum(
            "hqk,khd->qhd", attend_weights, value_tile, preferred_element_type=jnp.float32
        )

    return lax.map(per_tile, jnp.arange(tok_rows // tile_rows, dtype=jnp.int32)).reshape(
        tok_rows, heads_here, HDIM
    )


def memory_attention(queries, fetched):
    tok_rows, features = queries.shape
    heads_here = features // HDIM
    block_count = tok_rows // QBLK
    score_scale = 1.0 / math.sqrt(HDIM)
    query_blocks = queries.reshape(block_count, QBLK, heads_here, HDIM)
    key_blocks = fetched[:, 0].reshape(block_count, TOPM * MROWS, heads_here, HDIM)
    value_blocks = fetched[:, 1].reshape(block_count, TOPM * MROWS, heads_here, HDIM)
    scores = (
        jnp.einsum("bqhd,bkhd->bhqk", query_blocks, key_blocks, preferred_element_type=jnp.float32)
        * score_scale
    )
    attend_weights = masked_softmax(scores, jnp.ones(scores.shape, dtype=bool))
    remote = jnp.einsum(
        "bhqk,bkhd->bqhd", attend_weights, value_blocks, preferred_element_type=jnp.float32
    )
    return remote.reshape(tok_rows, heads_here, HDIM)


def mixed_memory_attention(queries, returned, shared, local_part, mixing_row, slot_owner, slot_shared):
    tok_rows, features = queries.shape
    heads_here = features // HDIM
    block_count = tok_rows // QBLK
    score_scale = 1.0 / math.sqrt(HDIM)

    def kernel(owner_ref, flag_ref, q_ref, r0, r1, r2, r3, sh_ref, loc_ref, mix_ref, out_ref):
        c = pl.program_id(0)
        fetched = (r0, r1, r2, r3)
        key_parts = []
        value_parts = []
        for j in range(TOPM):
            use_shared = flag_ref[c * TOPM + j] == 1
            key_parts.append(jnp.where(use_shared, sh_ref[0], fetched[j][0, 0]))
            value_parts.append(jnp.where(use_shared, sh_ref[1], fetched[j][0, 1]))
        key_tile = jnp.concatenate(key_parts, axis=0)
        value_tile = jnp.concatenate(value_parts, axis=0)
        query_tile = q_ref[...]
        for h in range(heads_here):
            cols = slice(h * HDIM, (h + 1) * HDIM)
            scores = lax.dot_general(query_tile[:, cols], key_tile[:, cols], (((1,), (1,)), ((), ())),
                                     preferred_element_type=jnp.float32) * score_scale
            row_max = jnp.max(scores, axis=-1, keepdims=True)
            weights = jnp.exp(scores - row_max)
            weights = (weights / jnp.sum(weights, axis=-1, keepdims=True)).astype(jnp.bfloat16)
            remote = jnp.dot(weights, value_tile[:, cols], preferred_element_type=jnp.float32)
            gate = mix_ref[:, cols]
            out_ref[:, cols] = (gate * remote + (1.0 - gate) * loc_ref[:, cols]).astype(jnp.bfloat16)

    def fetched_spec(j):
        return pl.BlockSpec((1, 2, MROWS, features), lambda c, owner, flag: (owner[c * TOPM + j], 0, 0, 0))

    grid_spec = pltpu.PrefetchScalarGridSpec(
        num_scalar_prefetch=2,
        grid=(block_count,),
        in_specs=[pl.BlockSpec((QBLK, features), lambda c, owner, flag: (c, 0))]
        + [fetched_spec(j) for j in range(TOPM)]
        + [
            pl.BlockSpec((2, MROWS, features), lambda c, owner, flag: (0, 0, 0)),
            pl.BlockSpec((QBLK, features), lambda c, owner, flag: (c, 0)),
            pl.BlockSpec((1, features), lambda c, owner, flag: (0, 0)),
        ],
        out_specs=pl.BlockSpec((QBLK, features), lambda c, owner, flag: (c, 0)),
    )
    return pl.pallas_call(
        kernel,
        grid_spec=grid_spec,
        out_shape=jax.ShapeDtypeStruct((tok_rows, features), jnp.bfloat16),
        compiler_params=pltpu.CompilerParams(dimension_semantics=("arbitrary",)),
    )(slot_owner, slot_shared, queries, returned, returned, returned, returned, shared, local_part, mixing_row)


def build_table(slot_index, offset, in_use, total_slots):
    matches = (jnp.arange(total_slots, dtype=jnp.int32)[:, None] == slot_index[None, :]) & in_use[
        None, :
    ]
    return jnp.sum(jnp.where(matches, offset[None, :] + 1, 0), axis=1) - 1


def on_device(queries, keys, values, memory_keys, memory_values, block_ids, gate_bias, out_weight):
    tok_rows, features = queries.shape
    owners = lax.axis_size("seq")
    groups = lax.axis_size("head")
    seq_index = lax.axis_index("seq")
    first_row = seq_index * tok_rows
    full_weight = lax.all_gather(out_weight, "head", axis=0, tiled=True)
    request_count = block_ids.shape[0] * block_ids.shape[1]
    wanted = block_ids.reshape(request_count)
    mem_dev = memory_keys.shape[0] // MROWS
    last_block = owners * mem_dev - 1
    owner_index = wanted // mem_dev
    offset = wanted % mem_dev
    is_last = wanted == last_block
    memory_store = jnp.stack(
        (
            memory_keys.reshape(mem_dev, MROWS, features),
            memory_values.reshape(mem_dev, MROWS, features),
        ),
        axis=1,
    )
    slot_table = build_table(owner_index, offset, jnp.logical_not(is_last), owners).reshape(owners, 1)
    edge_rows = jnp.stack((keys, values))
    before = passed_along(edge_rows, "seq", 1)
    asked_for = lax.all_to_all(slot_table, "seq", split_axis=0, concat_axis=0, tiled=True)
    outgoing = memory_store[jnp.maximum(asked_for[:, 0], 0)]
    before, outgoing = lax.optimization_barrier((before, outgoing))
    returned = lax.all_to_all(outgoing, "seq", split_axis=0, concat_axis=0, tiled=True)
    shared = lax.psum(
        jnp.where(seq_index == owners - 1, memory_store[mem_dev - 1], jnp.zeros_like(memory_store[0])),
        "seq",
    )
    local_part = window_attention(
        queries, jnp.concatenate([before[0], keys]), jnp.concatenate([before[1], values]), first_row
    )
    mixing_row = jnp.repeat(jax.nn.sigmoid(gate_bias), HDIM)[None, :]
    attended = mixed_memory_attention(
        queries,
        returned,
        shared,
        local_part.reshape(tok_rows, features),
        mixing_row,
        owner_index,
        is_last.astype(jnp.int32),
    )
    out_rows = tok_rows // groups
    gathered = lax.all_to_all(
        attended.reshape(groups, out_rows, features), "head", split_axis=0, concat_axis=0, tiled=True
    )
    partials = jnp.einsum(
        "gqf,gfn->gqn",
        gathered,
        full_weight.reshape(groups, features, full_weight.shape[1]),
        preferred_element_type=jnp.float32,
    ).astype(jnp.bfloat16)
    return jnp.sum(partials.astype(jnp.float32), axis=0).astype(jnp.bfloat16)


def solution(mesh):
    in_specs = (
        P("seq", "head"),
        P("seq", "head"),
        P("seq", "head"),
        P("seq", "head"),
        P("seq", "head"),
        P("seq", None),
        P("head"),
        P("head", None),
    )
    out_specs = P(("seq", "head"), None)
    return jax.shard_map(
        on_device, mesh=mesh, in_specs=in_specs, out_specs=out_specs, check_vma=False
    )
```

```python
import math

import jax
import jax.numpy as jnp
from jax import lax
from jax.experimental import pallas as pl
from jax.experimental.pallas import tpu as pltpu
from jax.sharding import PartitionSpec as P

HDIM = 128
WINDOW = 1024
QBLK = 128
MROWS = 64
TOPM = 4


NEG_FILL = -1e30


def passed_along(value, axis, steps):
    count = lax.axis_size(axis)
    leading, last = (max(0, -steps), min(count, count - steps))
    return lax.ppermute(value, axis, [(source, source + steps) for source in range(leading, last)])


def masked_softmax(scores, allowed):
    row_max = jnp.max(jnp.where(allowed, scores, NEG_FILL), axis=-1, keepdims=True)
    weights = jnp.where(allowed, jnp.exp(scores - row_max), 0.0)
    return (weights / jnp.sum(weights, axis=-1, keepdims=True)).astype(jnp.bfloat16)


def window_attention(queries, ext_keys, ext_values, first_row):
    tok_rows, features = queries.shape
    heads_here = features // HDIM
    tile_rows = math.gcd(tok_rows, 512)
    key_span = tile_rows + WINDOW
    score_scale = 1.0 / math.sqrt(HDIM)

    def per_tile(step_index):
        row_start = step_index * tile_rows
        query_tile = lax.dynamic_slice_in_dim(queries, row_start, tile_rows, 0).reshape(
            tile_rows, heads_here, HDIM
        )
        key_tile = lax.dynamic_slice_in_dim(ext_keys, row_start, key_span, 0).reshape(
            key_span, heads_here, HDIM
        )
        value_tile = lax.dynamic_slice_in_dim(ext_values, row_start, key_span, 0).reshape(
            key_span, heads_here, HDIM
        )
        scores = (
            jnp.einsum("qhd,khd->hqk", query_tile, key_tile, preferred_element_type=jnp.float32)
            * score_scale
        )
        query_pos = first_row + row_start + jnp.arange(tile_rows, dtype=jnp.int32)
        key_pos = first_row + row_start - WINDOW + jnp.arange(key_span, dtype=jnp.int32)
        allowed = (
            (key_pos[None, :] <= query_pos[:, None])
            & (key_pos[None, :] > query_pos[:, None] - WINDOW)
            & (key_pos[None, :] >= 0)
        )
        attend_weights = masked_softmax(scores, allowed[None])
        return jnp.einsum(
            "hqk,khd->qhd", attend_weights, value_tile, preferred_element_type=jnp.float32
        )

    return lax.map(per_tile, jnp.arange(tok_rows // tile_rows, dtype=jnp.int32)).reshape(
        tok_rows, heads_here, HDIM
    )


def memory_attention(queries, fetched):
    tok_rows, features = queries.shape
    heads_here = features // HDIM
    block_count = tok_rows // QBLK
    score_scale = 1.0 / math.sqrt(HDIM)
    query_blocks = queries.reshape(block_count, QBLK, heads_here, HDIM)
    key_blocks = fetched[:, 0].reshape(block_count, TOPM * MROWS, heads_here, HDIM)
    value_blocks = fetched[:, 1].reshape(block_count, TOPM * MROWS, heads_here, HDIM)
    scores = (
        jnp.einsum("bqhd,bkhd->bhqk", query_blocks, key_blocks, preferred_element_type=jnp.float32)
        * score_scale
    )
    attend_weights = masked_softmax(scores, jnp.ones(scores.shape, dtype=bool))
    remote = jnp.einsum(
        "bhqk,bkhd->bqhd", attend_weights, value_blocks, preferred_element_type=jnp.float32
    )
    return remote.reshape(tok_rows, heads_here, HDIM)


def mixed_memory_attention(queries, returned, shared, local_part, mixing_row, block_order, slot_owner, slot_shared, written, first, count):
    tok_rows, features = queries.shape
    heads_here = features // HDIM
    score_scale = 1.0 / math.sqrt(HDIM)

    def kernel(order_ref, owner_ref, flag_ref, q_ref, r0, r1, r2, r3, sh_ref, loc_ref, mix_ref, *rest):
        out_ref = rest[-1]
        c = order_ref[first + pl.program_id(0)]
        fetched = (r0, r1, r2, r3)
        key_parts = []
        value_parts = []
        for j in range(TOPM):
            use_shared = flag_ref[c * TOPM + j] == 1
            key_parts.append(jnp.where(use_shared, sh_ref[0], fetched[j][0, 0]))
            value_parts.append(jnp.where(use_shared, sh_ref[1], fetched[j][0, 1]))
        key_tile = jnp.concatenate(key_parts, axis=0)
        value_tile = jnp.concatenate(value_parts, axis=0)
        query_tile = q_ref[...]
        for h in range(heads_here):
            cols = slice(h * HDIM, (h + 1) * HDIM)
            scores = (
                lax.dot_general(
                    query_tile[:, cols],
                    key_tile[:, cols],
                    (((1,), (1,)), ((), ())),
                    preferred_element_type=jnp.float32,
                )
                * score_scale
            )
            row_max = jnp.max(scores, axis=-1, keepdims=True)
            weights = jnp.exp(scores - row_max)
            weights = (weights / jnp.sum(weights, axis=-1, keepdims=True)).astype(jnp.bfloat16)
            remote = jnp.dot(weights, value_tile[:, cols], preferred_element_type=jnp.float32)
            gate = mix_ref[:, cols]
            out_ref[:, cols] = (gate * remote + (1.0 - gate) * loc_ref[:, cols]).astype(jnp.bfloat16)

    def rows_spec():
        return pl.BlockSpec((QBLK, features), lambda i, order, owner, flag: (order[first + i], 0))

    def fetched_spec(j):
        return pl.BlockSpec(
            (1, 2, MROWS, features),
            lambda i, order, owner, flag: (owner[order[first + i] * TOPM + j], 0, 0, 0),
        )

    in_specs = (
        [rows_spec()]
        + [fetched_spec(j) for j in range(TOPM)]
        + [
            pl.BlockSpec((2, MROWS, features), lambda i, order, owner, flag: (0, 0, 0)),
            rows_spec(),
            pl.BlockSpec((1, features), lambda i, order, owner, flag: (0, 0)),
        ]
    )
    operands = [queries, returned, returned, returned, returned, shared, local_part, mixing_row]
    aliases = {}
    if written is not None:
        in_specs.append(pl.BlockSpec(memory_space=pl.ANY))
        operands.append(written)
        aliases = {3 + len(operands) - 1: 0}
    grid_spec = pltpu.PrefetchScalarGridSpec(
        num_scalar_prefetch=3,
        grid=(count,),
        in_specs=in_specs,
        out_specs=rows_spec(),
    )
    return pl.pallas_call(
        kernel,
        grid_spec=grid_spec,
        out_shape=jax.ShapeDtypeStruct((tok_rows, features), jnp.bfloat16),
        input_output_aliases=aliases,
        compiler_params=pltpu.CompilerParams(dimension_semantics=("arbitrary",)),
    )(block_order, slot_owner, slot_shared, *operands)


def build_table(slot_index, offset, in_use, total_slots):
    matches = (jnp.arange(total_slots, dtype=jnp.int32)[:, None] == slot_index[None, :]) & in_use[
        None, :
    ]
    return jnp.sum(jnp.where(matches, offset[None, :] + 1, 0), axis=1) - 1


def on_device(queries, keys, values, memory_keys, memory_values, block_ids, gate_bias, out_weight):
    tok_rows, features = queries.shape
    owners = lax.axis_size("seq")
    groups = lax.axis_size("head")
    seq_index = lax.axis_index("seq")
    first_row = seq_index * tok_rows
    full_weight = lax.all_gather(out_weight, "head", axis=0, tiled=True)
    request_count = block_ids.shape[0] * block_ids.shape[1]
    wanted = block_ids.reshape(request_count)
    mem_dev = memory_keys.shape[0] // MROWS
    last_block = owners * mem_dev - 1
    owner_index = wanted // mem_dev
    offset = wanted % mem_dev
    is_last = wanted == last_block
    memory_store = jnp.stack(
        (
            memory_keys.reshape(mem_dev, MROWS, features),
            memory_values.reshape(mem_dev, MROWS, features),
        ),
        axis=1,
    )
    slot_table = build_table(owner_index, offset, jnp.logical_not(is_last), owners).reshape(owners, 1)
    edge_rows = jnp.stack((keys, values))
    before = passed_along(edge_rows, "seq", 1)
    asked_for = lax.all_to_all(slot_table, "seq", split_axis=0, concat_axis=0, tiled=True)
    outgoing = memory_store[jnp.maximum(asked_for[:, 0], 0)]
    before, outgoing = lax.optimization_barrier((before, outgoing))
    returned = lax.all_to_all(outgoing, "seq", split_axis=0, concat_axis=0, tiled=True)
    shared = lax.psum(
        jnp.where(seq_index == owners - 1, memory_store[mem_dev - 1], jnp.zeros_like(memory_store[0])),
        "seq",
    )
    local_part = window_attention(
        queries, jnp.concatenate([before[0], keys]), jnp.concatenate([before[1], values]), first_row
    )
    mixing_row = jnp.repeat(jax.nn.sigmoid(gate_bias), HDIM)[None, :]
    block_count = tok_rows // QBLK
    uses_shared = jnp.any(is_last.reshape(block_count, TOPM), axis=1)
    block_order = jnp.argsort(uses_shared.astype(jnp.int32), stable=True).astype(jnp.int32)
    flags = is_last.astype(jnp.int32)
    local_rows = local_part.reshape(tok_rows, features)
    no_shared = jnp.zeros_like(shared)
    attended = mixed_memory_attention(
        queries, returned, no_shared, local_rows, mixing_row, block_order, owner_index, flags,
        None, 0, block_count - 1,
    )
    attended = mixed_memory_attention(
        queries, returned, shared, local_rows, mixing_row, block_order, owner_index, flags,
        attended, block_count - 1, 1,
    )
    out_rows = tok_rows // groups
    gathered = lax.all_to_all(
        attended.reshape(groups, out_rows, features), "head", split_axis=0, concat_axis=0, tiled=True
    )
    partials = jnp.einsum(
        "gqf,gfn->gqn",
        gathered,
        full_weight.reshape(groups, features, full_weight.shape[1]),
        preferred_element_type=jnp.float32,
    ).astype(jnp.bfloat16)
    return jnp.sum(partials.astype(jnp.float32), axis=0).astype(jnp.bfloat16)


def solution(mesh):
    in_specs = (
        P("seq", "head"),
        P("seq", "head"),
        P("seq", "head"),
        P("seq", "head"),
        P("seq", "head"),
        P("seq", None),
        P("head"),
        P("head", None),
    )
    out_specs = P(("seq", "head"), None)
    return jax.shard_map(
        on_device, mesh=mesh, in_specs=in_specs, out_specs=out_specs, check_vma=False
    )
```

```python
import math

import jax
import jax.numpy as jnp
from jax import lax
from jax.experimental import pallas as pl
from jax.experimental.pallas import tpu as pltpu
from jax.sharding import PartitionSpec as P


HDIM = 128
WINDOW = 1024
QBLK = 128
MROWS = 64
TOPM = 4


NEG_FILL = -1e30


def passed_along(value, axis, steps):
    count = lax.axis_size(axis)
    leading, last = (max(0, -steps), min(count, count - steps))
    return lax.ppermute(value, axis, [(source, source + steps) for source in range(leading, last)])


def masked_softmax(scores, allowed):
    row_max = jnp.max(jnp.where(allowed, scores, NEG_FILL), axis=-1, keepdims=True)
    weights = jnp.where(allowed, jnp.exp(scores - row_max), 0.0)
    return (weights / jnp.sum(weights, axis=-1, keepdims=True)).astype(jnp.bfloat16)


def window_attention(queries, ext_keys, ext_values, first_row):
    tok_rows, features = queries.shape
    heads_here = features // HDIM
    tile_rows = math.gcd(tok_rows, 512)
    key_span = tile_rows + WINDOW
    score_scale = 1.0 / math.sqrt(HDIM)

    def per_tile(step_index):
        row_start = step_index * tile_rows
        query_tile = lax.dynamic_slice_in_dim(queries, row_start, tile_rows, 0).reshape(
            tile_rows, heads_here, HDIM
        )
        key_tile = lax.dynamic_slice_in_dim(ext_keys, row_start, key_span, 0).reshape(
            key_span, heads_here, HDIM
        )
        value_tile = lax.dynamic_slice_in_dim(ext_values, row_start, key_span, 0).reshape(
            key_span, heads_here, HDIM
        )
        scores = (
            jnp.einsum("qhd,khd->hqk", query_tile, key_tile, preferred_element_type=jnp.float32)
            * score_scale
        )
        query_pos = first_row + row_start + jnp.arange(tile_rows, dtype=jnp.int32)
        key_pos = first_row + row_start - WINDOW + jnp.arange(key_span, dtype=jnp.int32)
        allowed = (
            (key_pos[None, :] <= query_pos[:, None])
            & (key_pos[None, :] > query_pos[:, None] - WINDOW)
            & (key_pos[None, :] >= 0)
        )
        attend_weights = masked_softmax(scores, allowed[None])
        return jnp.einsum(
            "hqk,khd->qhd", attend_weights, value_tile, preferred_element_type=jnp.float32
        )

    return lax.map(per_tile, jnp.arange(tok_rows // tile_rows, dtype=jnp.int32)).reshape(
        tok_rows, heads_here, HDIM
    )


def mixed_memory_attention(queries, returned, shared, local_part, mixing_row, block_order, slot_owner, slot_shared, written, first, count):
    tok_rows, features = queries.shape
    heads_here = features // HDIM
    score_scale = 1.0 / math.sqrt(HDIM)

    def kernel(order_ref, owner_ref, flag_ref, q_ref, r0, r1, r2, r3, sh_ref, loc_ref, mix_ref, *rest):
        out_ref = rest[-1]
        c = order_ref[first + pl.program_id(0)]
        fetched = (r0, r1, r2, r3)
        key_parts = []
        value_parts = []
        for j in range(TOPM):
            use_shared = flag_ref[c * TOPM + j] == 1
            key_parts.append(jnp.where(use_shared, sh_ref[0], fetched[j][0, 0]))
            value_parts.append(jnp.where(use_shared, sh_ref[1], fetched[j][0, 1]))
        key_tile = jnp.concatenate(key_parts, axis=0)
        value_tile = jnp.concatenate(value_parts, axis=0)
        query_tile = q_ref[...]
        for h in range(heads_here):
            cols = slice(h * HDIM, (h + 1) * HDIM)
            scores = (
                lax.dot_general(
                    query_tile[:, cols],
                    key_tile[:, cols],
                    (((1,), (1,)), ((), ())),
                    preferred_element_type=jnp.float32,
                )
                * score_scale
            )
            row_max = jnp.max(scores, axis=-1, keepdims=True)
            weights = jnp.exp(scores - row_max)
            weights = (weights / jnp.sum(weights, axis=-1, keepdims=True)).astype(jnp.bfloat16)
            remote = jnp.dot(weights, value_tile[:, cols], preferred_element_type=jnp.float32)
            gate = mix_ref[:, cols]
            out_ref[:, cols] = (gate * remote + (1.0 - gate) * loc_ref[:, cols]).astype(jnp.bfloat16)

    def rows_spec():
        return pl.BlockSpec((QBLK, features), lambda i, order, owner, flag: (order[first + i], 0))

    def fetched_spec(j):
        return pl.BlockSpec(
            (1, 2, MROWS, features),
            lambda i, order, owner, flag: (owner[order[first + i] * TOPM + j], 0, 0, 0),
        )

    in_specs = (
        [rows_spec()]
        + [fetched_spec(j) for j in range(TOPM)]
        + [
            pl.BlockSpec((2, MROWS, features), lambda i, order, owner, flag: (0, 0, 0)),
            rows_spec(),
            pl.BlockSpec((1, features), lambda i, order, owner, flag: (0, 0)),
        ]
    )
    operands = [queries, returned, returned, returned, returned, shared, local_part, mixing_row]
    aliases = {}
    if written is not None:
        in_specs.append(pl.BlockSpec(memory_space=pl.ANY))
        operands.append(written)
        aliases = {3 + len(operands) - 1: 0}
    grid_spec = pltpu.PrefetchScalarGridSpec(
        num_scalar_prefetch=3,
        grid=(count,),
        in_specs=in_specs,
        out_specs=rows_spec(),
    )
    return pl.pallas_call(
        kernel,
        grid_spec=grid_spec,
        out_shape=jax.ShapeDtypeStruct((tok_rows, features), jnp.bfloat16),
        input_output_aliases=aliases,
        compiler_params=pltpu.CompilerParams(dimension_semantics=("arbitrary",)),
    )(block_order, slot_owner, slot_shared, *operands)


def build_table(slot_index, offset, in_use, total_slots):
    matches = (jnp.arange(total_slots, dtype=jnp.int32)[:, None] == slot_index[None, :]) & in_use[
        None, :
    ]
    return jnp.sum(jnp.where(matches, offset[None, :] + 1, 0), axis=1) - 1


def layer(queries, keys, values, memory_keys, memory_values, block_ids, gate_bias, out_weight):
    tok_rows, features = queries.shape
    owners = lax.axis_size("seq")
    groups = lax.axis_size("head")
    seq_index = lax.axis_index("seq")
    first_row = seq_index * tok_rows
    full_weight = lax.all_gather(out_weight, "head", axis=0, tiled=True)
    request_count = block_ids.shape[0] * block_ids.shape[1]
    wanted = block_ids.reshape(request_count)
    mem_dev = memory_keys.shape[0] // MROWS
    last_block = owners * mem_dev - 1
    owner_index = wanted // mem_dev
    offset = wanted % mem_dev
    is_last = wanted == last_block
    memory_store = jnp.stack(
        (
            memory_keys.reshape(mem_dev, MROWS, features),
            memory_values.reshape(mem_dev, MROWS, features),
        ),
        axis=1,
    )
    slot_table = build_table(owner_index, offset, jnp.logical_not(is_last), owners).reshape(owners, 1)
    edge_rows = jnp.stack((keys, values))
    before = passed_along(edge_rows, "seq", 1)
    asked_for = lax.all_to_all(slot_table, "seq", split_axis=0, concat_axis=0, tiled=True)
    outgoing = memory_store[jnp.maximum(asked_for[:, 0], 0)]
    before, outgoing = lax.optimization_barrier((before, outgoing))
    returned = lax.all_to_all(outgoing, "seq", split_axis=0, concat_axis=0, tiled=True)
    shared = lax.psum(
      jnp.where(seq_index == owners - 1, memory_store[mem_dev - 1], jnp.zeros_like(memory_store[0])),
      "seq",
    )
    local_part = window_attention(
        queries, jnp.concatenate([before[0], keys]), jnp.concatenate([before[1], values]), first_row
    )
    mixing_row = jnp.repeat(jax.nn.sigmoid(gate_bias), HDIM)[None, :]
    block_count = tok_rows // QBLK
    uses_shared = jnp.any(is_last.reshape(block_count, TOPM), axis=1)
    block_order = jnp.argsort(uses_shared.astype(jnp.int32), stable=True).astype(jnp.int32)
    flags = is_last.astype(jnp.int32)
    local_rows = local_part.reshape(tok_rows, features)
    no_shared = jnp.zeros_like(shared)
    attended = mixed_memory_attention(
        queries, returned, no_shared, local_rows, mixing_row, block_order, owner_index, flags,
        None, 0, block_count - 1,
    )
    attended = mixed_memory_attention(
        queries, returned, shared, local_rows, mixing_row, block_order, owner_index, flags,
        attended, block_count - 1, 1,
    )
    out_rows = tok_rows // groups
    gathered = lax.all_to_all(
        attended.reshape(groups, out_rows, features), "head", split_axis=0, concat_axis=0, tiled=True
    )
    partials = jnp.einsum(
        "gqf,gfn->gqn",
        gathered,
        full_weight.reshape(groups, features, full_weight.shape[1]),
        preferred_element_type=jnp.float32,
    ).astype(jnp.bfloat16)
    return jnp.sum(partials.astype(jnp.float32), axis=0).astype(jnp.bfloat16)


def solution(mesh):
    in_specs = (
        P("seq", "head"),
        P("seq", "head"),
        P("seq", "head"),
        P("seq", "head"),
        P("seq", "head"),
        P("seq", None),
        P("head"),
        P("head", None),
    )
    out_specs = P(("seq", "head"), None)
    return jax.shard_map(layer, mesh=mesh, in_specs=in_specs, out_specs=out_specs, check_vma=False)
```

```python
import math

import jax
import jax.numpy as jnp
from jax import lax
from jax.experimental import pallas as pl
from jax.experimental.pallas import tpu as pltpu
from jax.sharding import PartitionSpec as P


HDIM = 128
WINDOW = 1024
QBLK = 128
MROWS = 64
TOPM = 4


NEG_FILL = -1e30


def passed_along(value, axis, steps):
    count = lax.axis_size(axis)
    leading, last = (max(0, -steps), min(count, count - steps))
    return lax.ppermute(value, axis, [(source, source + steps) for source in range(leading, last)])


def masked_softmax(scores, allowed):
    row_max = jnp.max(jnp.where(allowed, scores, NEG_FILL), axis=-1, keepdims=True)
    weights = jnp.where(allowed, jnp.exp(scores - row_max), 0.0)
    return (weights / jnp.sum(weights, axis=-1, keepdims=True)).astype(jnp.bfloat16)


def window_attention(queries, ext_keys, ext_values, first_row):
    tok_rows, features = queries.shape
    heads_here = features // HDIM
    tile_rows = math.gcd(tok_rows, 512)
    key_span = tile_rows + WINDOW
    score_scale = 1.0 / math.sqrt(HDIM)

    def per_tile(step_index):
        row_start = step_index * tile_rows
        query_tile = lax.dynamic_slice_in_dim(queries, row_start, tile_rows, 0).reshape(
            tile_rows, heads_here, HDIM
        )
        key_tile = lax.dynamic_slice_in_dim(ext_keys, row_start, key_span, 0).reshape(
            key_span, heads_here, HDIM
        )
        value_tile = lax.dynamic_slice_in_dim(ext_values, row_start, key_span, 0).reshape(
            key_span, heads_here, HDIM
        )
        scores = (
            jnp.einsum("qhd,khd->hqk", query_tile, key_tile, preferred_element_type=jnp.float32)
            * score_scale
        )
        query_pos = first_row + row_start + jnp.arange(tile_rows, dtype=jnp.int32)
        key_pos = first_row + row_start - WINDOW + jnp.arange(key_span, dtype=jnp.int32)
        allowed = (
            (key_pos[None, :] <= query_pos[:, None])
            & (key_pos[None, :] > query_pos[:, None] - WINDOW)
            & (key_pos[None, :] >= 0)
        )
        attend_weights = masked_softmax(scores, allowed[None])
        return jnp.einsum(
            "hqk,khd->qhd", attend_weights, value_tile, preferred_element_type=jnp.float32
        )

    return lax.map(per_tile, jnp.arange(tok_rows // tile_rows, dtype=jnp.int32)).reshape(
        tok_rows, heads_here, HDIM
    )


def mixed_memory_attention(queries, returned, shared, local_part, mixing_row, block_order, slot_owner, slot_shared, written, first, count):
    tok_rows, features = queries.shape
    heads_here = features // HDIM
    score_scale = 1.0 / math.sqrt(HDIM)

    def kernel(order_ref, owner_ref, flag_ref, q_ref, r0, r1, r2, r3, sh_ref, loc_ref, mix_ref, *rest):
        out_ref = rest[-1]
        c = order_ref[first + pl.program_id(0)]
        fetched = (r0, r1, r2, r3)
        key_parts = []
        value_parts = []
        for j in range(TOPM):
            use_shared = flag_ref[c * TOPM + j] == 1
            key_parts.append(jnp.where(use_shared, sh_ref[0], fetched[j][0, 0]))
            value_parts.append(jnp.where(use_shared, sh_ref[1], fetched[j][0, 1]))
        key_tile = jnp.concatenate(key_parts, axis=0)
        value_tile = jnp.concatenate(value_parts, axis=0)
        query_tile = q_ref[...]
        for h in range(heads_here):
            cols = slice(h * HDIM, (h + 1) * HDIM)
            scores = (
                lax.dot_general(
                    query_tile[:, cols],
                    key_tile[:, cols],
                    (((1,), (1,)), ((), ())),
                    preferred_element_type=jnp.float32,
                )
                * score_scale
            )
            row_max = jnp.max(scores, axis=-1, keepdims=True)
            weights = jnp.exp(scores - row_max)
            weights = (weights / jnp.sum(weights, axis=-1, keepdims=True)).astype(jnp.bfloat16)
            remote = jnp.dot(weights, value_tile[:, cols], preferred_element_type=jnp.float32)
            gate = mix_ref[:, cols]
            out_ref[:, cols] = (gate * remote + (1.0 - gate) * loc_ref[:, cols]).astype(jnp.bfloat16)

    def rows_spec():
        return pl.BlockSpec((QBLK, features), lambda i, order, owner, flag: (order[first + i], 0))

    def fetched_spec(j):
        return pl.BlockSpec(
            (1, 2, MROWS, features),
            lambda i, order, owner, flag: (owner[order[first + i] * TOPM + j], 0, 0, 0),
        )

    in_specs = (
        [rows_spec()]
        + [fetched_spec(j) for j in range(TOPM)]
        + [
            pl.BlockSpec((2, MROWS, features), lambda i, order, owner, flag: (0, 0, 0)),
            rows_spec(),
            pl.BlockSpec((1, features), lambda i, order, owner, flag: (0, 0)),
        ]
    )
    operands = [queries, returned, returned, returned, returned, shared, local_part, mixing_row]
    aliases = {}
    if written is not None:
        in_specs.append(pl.BlockSpec(memory_space=pl.ANY))
        operands.append(written)
        aliases = {3 + len(operands) - 1: 0}
    grid_spec = pltpu.PrefetchScalarGridSpec(
        num_scalar_prefetch=3,
        grid=(count,),
        in_specs=in_specs,
        out_specs=rows_spec(),
    )
    return pl.pallas_call(
        kernel,
        grid_spec=grid_spec,
        out_shape=jax.ShapeDtypeStruct((tok_rows, features), jnp.bfloat16),
        input_output_aliases=aliases,
        compiler_params=pltpu.CompilerParams(dimension_semantics=("arbitrary",)),
    )(block_order, slot_owner, slot_shared, *operands)


def build_table(slot_index, offset, in_use, total_slots):
    matches = (jnp.arange(total_slots, dtype=jnp.int32)[:, None] == slot_index[None, :]) & in_use[
        None, :
    ]
    return jnp.sum(jnp.where(matches, offset[None, :] + 1, 0), axis=1) - 1


def layer(queries, keys, values, memory_keys, memory_values, block_ids, gate_bias, out_weight):
    tok_rows, features = queries.shape
    owners = lax.axis_size("seq")
    groups = lax.axis_size("head")
    seq_index = lax.axis_index("seq")
    first_row = seq_index * tok_rows
    full_weight = lax.all_gather(out_weight, "head", axis=0, tiled=True)
    request_count = block_ids.shape[0] * block_ids.shape[1]
    wanted = block_ids.reshape(request_count)
    mem_dev = memory_keys.shape[0] // MROWS
    last_block = owners * mem_dev - 1
    owner_index = wanted // mem_dev
    offset = wanted % mem_dev
    is_last = wanted == last_block
    memory_store = jnp.stack(
        (
            memory_keys.reshape(mem_dev, MROWS, features),
            memory_values.reshape(mem_dev, MROWS, features),
        ),
        axis=1,
    )
    slot_table = build_table(owner_index, offset, jnp.logical_not(is_last), owners).reshape(owners, 1)
    edge_rows = jnp.stack((keys, values))
    before = passed_along(edge_rows, "seq", 1)
    asked_for = lax.all_to_all(slot_table, "seq", split_axis=0, concat_axis=0, tiled=True)
    outgoing = memory_store[jnp.maximum(asked_for[:, 0], 0)]
    before, outgoing = lax.optimization_barrier((before, outgoing))
    returned = lax.all_to_all(outgoing, "seq", split_axis=0, concat_axis=0, tiled=True)
    shared = lax.psum(
      jnp.where(seq_index == owners - 1, memory_store[mem_dev - 1], jnp.zeros_like(memory_store[0])),
      "seq",
    )
    local_part = window_attention(
        queries, jnp.concatenate([before[0], keys]), jnp.concatenate([before[1], values]), first_row
    )
    mixing_row = jnp.repeat(jax.nn.sigmoid(gate_bias), HDIM)[None, :]
    block_count = tok_rows // QBLK
    block_order = jnp.arange(block_count, dtype=jnp.int32)
    attended = mixed_memory_attention(
        queries, returned, shared, local_part.reshape(tok_rows, features), mixing_row, block_order,
        owner_index, is_last.astype(jnp.int32), None, 0, block_count,
    )
    out_rows = tok_rows // groups
    gathered = lax.all_to_all(
        attended.reshape(groups, out_rows, features), "head", split_axis=0, concat_axis=0, tiled=True
    )
    partials = jnp.einsum(
        "gqf,gfn->gqn",
        gathered,
        full_weight.reshape(groups, features, full_weight.shape[1]),
        preferred_element_type=jnp.float32,
    ).astype(jnp.bfloat16)
    return jnp.sum(partials.astype(jnp.float32), axis=0).astype(jnp.bfloat16)


def solution(mesh):
    in_specs = (
        P("seq", "head"),
        P("seq", "head"),
        P("seq", "head"),
        P("seq", "head"),
        P("seq", "head"),
        P("seq", None),
        P("head"),
        P("head", None),
    )
    out_specs = P(("seq", "head"), None)
    return jax.shard_map(layer, mesh=mesh, in_specs=in_specs, out_specs=out_specs, check_vma=False)
```

```python
import math

import jax
import jax.numpy as jnp
from jax import lax
from jax.experimental import pallas as pl
from jax.experimental.pallas import tpu as pltpu
from jax.sharding import PartitionSpec as P


HDIM = 128
WINDOW = 1024
QBLK = 128
MROWS = 64
TOPM = 4


NEG_FILL = -1e30


def passed_along(value, axis, steps):
    count = lax.axis_size(axis)
    leading, last = (max(0, -steps), min(count, count - steps))
    return lax.ppermute(value, axis, [(source, source + steps) for source in range(leading, last)])


def masked_softmax(scores, allowed):
    row_max = jnp.max(jnp.where(allowed, scores, NEG_FILL), axis=-1, keepdims=True)
    weights = jnp.where(allowed, jnp.exp(scores - row_max), 0.0)
    return (weights / jnp.sum(weights, axis=-1, keepdims=True)).astype(jnp.bfloat16)


def window_attention(queries, ext_keys, ext_values, first_row):
    tok_rows, features = queries.shape
    heads_here = features // HDIM
    tile_rows = math.gcd(tok_rows, 512)
    key_span = tile_rows + WINDOW
    score_scale = 1.0 / math.sqrt(HDIM)

    def per_tile(step_index):
        row_start = step_index * tile_rows
        query_tile = lax.dynamic_slice_in_dim(queries, row_start, tile_rows, 0).reshape(
            tile_rows, heads_here, HDIM
        )
        key_tile = lax.dynamic_slice_in_dim(ext_keys, row_start, key_span, 0).reshape(
            key_span, heads_here, HDIM
        )
        value_tile = lax.dynamic_slice_in_dim(ext_values, row_start, key_span, 0).reshape(
            key_span, heads_here, HDIM
        )
        scores = (
            jnp.einsum("qhd,khd->hqk", query_tile, key_tile, preferred_element_type=jnp.float32)
            * score_scale
        )
        query_pos = first_row + row_start + jnp.arange(tile_rows, dtype=jnp.int32)
        key_pos = first_row + row_start - WINDOW + jnp.arange(key_span, dtype=jnp.int32)
        allowed = (
            (key_pos[None, :] <= query_pos[:, None])
            & (key_pos[None, :] > query_pos[:, None] - WINDOW)
            & (key_pos[None, :] >= 0)
        )
        attend_weights = masked_softmax(scores, allowed[None])
        return jnp.einsum(
            "hqk,khd->qhd", attend_weights, value_tile, preferred_element_type=jnp.float32
        )

    return lax.map(per_tile, jnp.arange(tok_rows // tile_rows, dtype=jnp.int32)).reshape(
        tok_rows, heads_here, HDIM
    )


def mixed_memory_attention(queries, returned, shared, local_part, mixing_row, block_order, slot_owner, slot_shared, written, first, count):
    tok_rows, features = queries.shape
    heads_here = features // HDIM
    score_scale = 1.0 / math.sqrt(HDIM)

    def kernel(order_ref, owner_ref, flag_ref, q_ref, r0, r1, r2, r3, sh_ref, loc_ref, mix_ref, *rest):
        out_ref = rest[-1]
        c = order_ref[first + pl.program_id(0)]
        fetched = (r0, r1, r2, r3)
        key_parts = []
        value_parts = []
        for j in range(TOPM):
            use_shared = flag_ref[c * TOPM + j] == 1
            key_parts.append(jnp.where(use_shared, sh_ref[0], fetched[j][0, 0]))
            value_parts.append(jnp.where(use_shared, sh_ref[1], fetched[j][0, 1]))
        key_tile = jnp.concatenate(key_parts, axis=0)
        value_tile = jnp.concatenate(value_parts, axis=0)
        query_tile = q_ref[...]
        for h in range(heads_here):
            cols = slice(h * HDIM, (h + 1) * HDIM)
            scores = (
                lax.dot_general(
                    query_tile[:, cols],
                    key_tile[:, cols],
                    (((1,), (1,)), ((), ())),
                    preferred_element_type=jnp.float32,
                )
                * score_scale
            )
            row_max = jnp.max(scores, axis=-1, keepdims=True)
            weights = jnp.exp(scores - row_max)
            weights = (weights / jnp.sum(weights, axis=-1, keepdims=True)).astype(jnp.bfloat16)
            remote = jnp.dot(weights, value_tile[:, cols], preferred_element_type=jnp.float32)
            gate = mix_ref[:, cols]
            out_ref[:, cols] = (gate * remote + (1.0 - gate) * loc_ref[:, cols]).astype(jnp.bfloat16)

    def rows_spec():
        return pl.BlockSpec((QBLK, features), lambda i, order, owner, flag: (order[first + i], 0))

    def fetched_spec(j):
        return pl.BlockSpec(
            (1, 2, MROWS, features),
            lambda i, order, owner, flag: (owner[order[first + i] * TOPM + j], 0, 0, 0),
        )

    in_specs = (
        [rows_spec()]
        + [fetched_spec(j) for j in range(TOPM)]
        + [
            pl.BlockSpec((2, MROWS, features), lambda i, order, owner, flag: (0, 0, 0)),
            rows_spec(),
            pl.BlockSpec((1, features), lambda i, order, owner, flag: (0, 0)),
        ]
    )
    operands = [queries, returned, returned, returned, returned, shared, local_part, mixing_row]
    aliases = {}
    if written is not None:
        in_specs.append(pl.BlockSpec(memory_space=pl.ANY))
        operands.append(written)
        aliases = {3 + len(operands) - 1: 0}
    grid_spec = pltpu.PrefetchScalarGridSpec(
        num_scalar_prefetch=3,
        grid=(count,),
        in_specs=in_specs,
        out_specs=rows_spec(),
    )
    return pl.pallas_call(
        kernel,
        grid_spec=grid_spec,
        out_shape=jax.ShapeDtypeStruct((tok_rows, features), jnp.bfloat16),
        input_output_aliases=aliases,
        compiler_params=pltpu.CompilerParams(dimension_semantics=("arbitrary",)),
    )(block_order, slot_owner, slot_shared, *operands)


def grouped_projection(gathered, weight):
    groups, rows, features = gathered.shape
    width = weight.shape[2]
    tile = math.gcd(width, 512)

    def kernel(a_ref, w_ref, o_ref):
        total = jnp.zeros((rows, tile), jnp.float32)
        for g in range(groups):
            part = jnp.dot(a_ref[g], w_ref[g], preferred_element_type=jnp.float32)
            total = total + part.astype(jnp.bfloat16).astype(jnp.float32)
        o_ref[...] = total.astype(jnp.bfloat16)

    return pl.pallas_call(
        kernel,
        grid=(width // tile,),
        in_specs=[
            pl.BlockSpec((groups, rows, features), lambda n: (0, 0, 0)),
            pl.BlockSpec((groups, features, tile), lambda n: (0, 0, n)),
        ],
        out_specs=pl.BlockSpec((rows, tile), lambda n: (0, n)),
        out_shape=jax.ShapeDtypeStruct((rows, width), jnp.bfloat16),
        compiler_params=pltpu.CompilerParams(dimension_semantics=("arbitrary",)),
    )(gathered, weight)


def build_table(slot_index, offset, in_use, total_slots):
    matches = (jnp.arange(total_slots, dtype=jnp.int32)[:, None] == slot_index[None, :]) & in_use[
        None, :
    ]
    return jnp.sum(jnp.where(matches, offset[None, :] + 1, 0), axis=1) - 1


def layer(queries, keys, values, memory_keys, memory_values, block_ids, gate_bias, out_weight):
    tok_rows, features = queries.shape
    owners = lax.axis_size("seq")
    groups = lax.axis_size("head")
    seq_index = lax.axis_index("seq")
    first_row = seq_index * tok_rows
    full_weight = lax.all_gather(out_weight, "head", axis=0, tiled=True)
    request_count = block_ids.shape[0] * block_ids.shape[1]
    wanted = block_ids.reshape(request_count)
    mem_dev = memory_keys.shape[0] // MROWS
    last_block = owners * mem_dev - 1
    owner_index = wanted // mem_dev
    offset = wanted % mem_dev
    is_last = wanted == last_block
    memory_store = jnp.stack(
        (
            memory_keys.reshape(mem_dev, MROWS, features),
            memory_values.reshape(mem_dev, MROWS, features),
        ),
        axis=1,
    )
    slot_table = build_table(owner_index, offset, jnp.logical_not(is_last), owners).reshape(owners, 1)
    edge_rows = jnp.stack((keys, values))
    before = passed_along(edge_rows, "seq", 1)
    asked_for = lax.all_to_all(slot_table, "seq", split_axis=0, concat_axis=0, tiled=True)
    outgoing = memory_store[jnp.maximum(asked_for[:, 0], 0)]
    before, outgoing = lax.optimization_barrier((before, outgoing))
    returned = lax.all_to_all(outgoing, "seq", split_axis=0, concat_axis=0, tiled=True)
    shared = lax.psum(
      jnp.where(seq_index == owners - 1, memory_store[mem_dev - 1], jnp.zeros_like(memory_store[0])),
      "seq",
    )
    local_part = window_attention(
        queries, jnp.concatenate([before[0], keys]), jnp.concatenate([before[1], values]), first_row
    )
    mixing_row = jnp.repeat(jax.nn.sigmoid(gate_bias), HDIM)[None, :]
    block_count = tok_rows // QBLK
    block_order = jnp.arange(block_count, dtype=jnp.int32)
    attended = mixed_memory_attention(
        queries, returned, shared, local_part.reshape(tok_rows, features), mixing_row, block_order,
        owner_index, is_last.astype(jnp.int32), None, 0, block_count,
    )
    out_rows = tok_rows // groups
    gathered = lax.all_to_all(
        attended.reshape(groups, out_rows, features), "head", split_axis=0, concat_axis=0, tiled=True
    )
    return grouped_projection(gathered, full_weight.reshape(groups, features, full_weight.shape[1]))


def solution(mesh):
    in_specs = (
        P("seq", "head"),
        P("seq", "head"),
        P("seq", "head"),
        P("seq", "head"),
        P("seq", "head"),
        P("seq", None),
        P("head"),
        P("head", None),
    )
    out_specs = P(("seq", "head"), None)
    return jax.shard_map(layer, mesh=mesh, in_specs=in_specs, out_specs=out_specs, check_vma=False)
```

```python
import math

import jax
import jax.numpy as jnp
from jax import lax
from jax.experimental import pallas as pl
from jax.experimental.pallas import tpu as pltpu
from jax.sharding import PartitionSpec as P


HDIM = 128
WINDOW = 1024
QBLK = 128
MROWS = 64
TOPM = 4


NEG_FILL = -1e30


def passed_along(value, axis, steps):
    count = lax.axis_size(axis)
    leading, last = (max(0, -steps), min(count, count - steps))
    return lax.ppermute(value, axis, [(source, source + steps) for source in range(leading, last)])


def masked_softmax(scores, allowed):
    row_max = jnp.max(jnp.where(allowed, scores, NEG_FILL), axis=-1, keepdims=True)
    weights = jnp.where(allowed, jnp.exp(scores - row_max), 0.0)
    return (weights / jnp.sum(weights, axis=-1, keepdims=True)).astype(jnp.bfloat16)


def window_attention(queries, ext_keys, ext_values, first_row):
    tok_rows, features = queries.shape
    heads_here = features // HDIM
    tile_rows = math.gcd(tok_rows, 512)
    key_span = tile_rows + WINDOW
    score_scale = 1.0 / math.sqrt(HDIM)

    def per_tile(step_index):
        row_start = step_index * tile_rows
        query_tile = lax.dynamic_slice_in_dim(queries, row_start, tile_rows, 0).reshape(
            tile_rows, heads_here, HDIM
        )
        key_tile = lax.dynamic_slice_in_dim(ext_keys, row_start, key_span, 0).reshape(
            key_span, heads_here, HDIM
        )
        value_tile = lax.dynamic_slice_in_dim(ext_values, row_start, key_span, 0).reshape(
            key_span, heads_here, HDIM
        )
        scores = (
            jnp.einsum("qhd,khd->hqk", query_tile, key_tile, preferred_element_type=jnp.float32)
            * score_scale
        )
        query_pos = first_row + row_start + jnp.arange(tile_rows, dtype=jnp.int32)
        key_pos = first_row + row_start - WINDOW + jnp.arange(key_span, dtype=jnp.int32)
        allowed = (
            (key_pos[None, :] <= query_pos[:, None])
            & (key_pos[None, :] > query_pos[:, None] - WINDOW)
            & (key_pos[None, :] >= 0)
        )
        attend_weights = masked_softmax(scores, allowed[None])
        return jnp.einsum(
            "hqk,khd->qhd", attend_weights, value_tile, preferred_element_type=jnp.float32
        )

    return lax.map(per_tile, jnp.arange(tok_rows // tile_rows, dtype=jnp.int32)).reshape(
        tok_rows, heads_here, HDIM
    )


def mixed_memory_attention(queries, returned, shared, local_part, mixing_row, block_order, slot_owner, slot_shared, written, first, count):
    tok_rows, features = queries.shape
    heads_here = features // HDIM
    score_scale = 1.0 / math.sqrt(HDIM)

    def kernel(order_ref, owner_ref, flag_ref, q_ref, r0, r1, r2, r3, sh_ref, loc_ref, mix_ref, *rest):
        out_ref = rest[-1]
        c = order_ref[first + pl.program_id(0)]
        fetched = (r0, r1, r2, r3)
        key_parts = []
        value_parts = []
        for j in range(TOPM):
            use_shared = flag_ref[c * TOPM + j] == 1
            key_parts.append(jnp.where(use_shared, sh_ref[0], fetched[j][0, 0]))
            value_parts.append(jnp.where(use_shared, sh_ref[1], fetched[j][0, 1]))
        key_tile = jnp.concatenate(key_parts, axis=0)
        value_tile = jnp.concatenate(value_parts, axis=0)
        query_tile = q_ref[...]
        for h in range(heads_here):
            cols = slice(h * HDIM, (h + 1) * HDIM)
            scores = (
                lax.dot_general(
                    query_tile[:, cols],
                    key_tile[:, cols],
                    (((1,), (1,)), ((), ())),
                    preferred_element_type=jnp.float32,
                )
                * score_scale
            )
            row_max = jnp.max(scores, axis=-1, keepdims=True)
            weights = jnp.exp(scores - row_max)
            weights = (weights / jnp.sum(weights, axis=-1, keepdims=True)).astype(jnp.bfloat16)
            remote = jnp.dot(weights, value_tile[:, cols], preferred_element_type=jnp.float32)
            gate = mix_ref[:, cols]
            out_ref[:, cols] = (gate * remote + (1.0 - gate) * loc_ref[:, cols]).astype(jnp.bfloat16)

    def rows_spec():
        return pl.BlockSpec((QBLK, features), lambda i, order, owner, flag: (order[first + i], 0))

    def fetched_spec(j):
        return pl.BlockSpec(
            (1, 2, MROWS, features),
            lambda i, order, owner, flag: (owner[order[first + i] * TOPM + j], 0, 0, 0),
        )

    in_specs = (
        [rows_spec()]
        + [fetched_spec(j) for j in range(TOPM)]
        + [
            pl.BlockSpec((2, MROWS, features), lambda i, order, owner, flag: (0, 0, 0)),
            rows_spec(),
            pl.BlockSpec((1, features), lambda i, order, owner, flag: (0, 0)),
        ]
    )
    operands = [queries, returned, returned, returned, returned, shared, local_part, mixing_row]
    aliases = {}
    if written is not None:
        in_specs.append(pl.BlockSpec(memory_space=pl.ANY))
        operands.append(written)
        aliases = {3 + len(operands) - 1: 0}
    grid_spec = pltpu.PrefetchScalarGridSpec(
        num_scalar_prefetch=3,
        grid=(count,),
        in_specs=in_specs,
        out_specs=rows_spec(),
    )
    return pl.pallas_call(
        kernel,
        grid_spec=grid_spec,
        out_shape=jax.ShapeDtypeStruct((tok_rows, features), jnp.bfloat16),
        input_output_aliases=aliases,
        compiler_params=pltpu.CompilerParams(dimension_semantics=("arbitrary",)),
    )(block_order, slot_owner, slot_shared, *operands)


def grouped_projection(own_part, gathered, weight, head_index):
    groups, rows, features = gathered.shape
    width = weight.shape[2]
    tile = math.gcd(width, 512)

    def kernel(head_ref, own_ref, *refs):
        parts = refs[: groups - 1]
        weights = refs[groups - 1 : 2 * (groups - 1)]
        o_ref = refs[-1]
        total = own_ref[...].astype(jnp.float32)
        for a_ref, w_ref in zip(parts, weights):
            part = jnp.dot(a_ref[0], w_ref[0], preferred_element_type=jnp.float32)
            total = total + part.astype(jnp.bfloat16).astype(jnp.float32)
        o_ref[...] = total.astype(jnp.bfloat16)

    def part_spec(k):
        return pl.BlockSpec((1, rows, features), lambda n, h: ((h[0] + k) % groups, 0, 0))

    def weight_spec(k):
        return pl.BlockSpec((1, features, tile), lambda n, h: ((h[0] + k) % groups, 0, n))

    others = range(1, groups)
    grid_spec = pltpu.PrefetchScalarGridSpec(
        num_scalar_prefetch=1,
        grid=(width // tile,),
        in_specs=[pl.BlockSpec((rows, tile), lambda n, h: (0, n))]
        + [part_spec(k) for k in others]
        + [weight_spec(k) for k in others],
        out_specs=pl.BlockSpec((rows, tile), lambda n, h: (0, n)),
    )
    return pl.pallas_call(
        kernel,
        grid_spec=grid_spec,
        out_shape=jax.ShapeDtypeStruct((rows, width), jnp.bfloat16),
        compiler_params=pltpu.CompilerParams(dimension_semantics=("arbitrary",)),
    )(head_index, own_part, *([gathered] * (groups - 1)), *([weight] * (groups - 1)))


def build_table(slot_index, offset, in_use, total_slots):
    matches = (jnp.arange(total_slots, dtype=jnp.int32)[:, None] == slot_index[None, :]) & in_use[
        None, :
    ]
    return jnp.sum(jnp.where(matches, offset[None, :] + 1, 0), axis=1) - 1


def layer(queries, keys, values, memory_keys, memory_values, block_ids, gate_bias, out_weight):
    tok_rows, features = queries.shape
    owners = lax.axis_size("seq")
    groups = lax.axis_size("head")
    seq_index = lax.axis_index("seq")
    first_row = seq_index * tok_rows
    full_weight = lax.all_gather(out_weight, "head", axis=0, tiled=True)
    request_count = block_ids.shape[0] * block_ids.shape[1]
    wanted = block_ids.reshape(request_count)
    mem_dev = memory_keys.shape[0] // MROWS
    last_block = owners * mem_dev - 1
    owner_index = wanted // mem_dev
    offset = wanted % mem_dev
    is_last = wanted == last_block
    memory_store = jnp.stack(
        (
            memory_keys.reshape(mem_dev, MROWS, features),
            memory_values.reshape(mem_dev, MROWS, features),
        ),
        axis=1,
    )
    slot_table = build_table(owner_index, offset, jnp.logical_not(is_last), owners).reshape(owners, 1)
    edge_rows = jnp.stack((keys, values))
    before = passed_along(edge_rows, "seq", 1)
    asked_for = lax.all_to_all(slot_table, "seq", split_axis=0, concat_axis=0, tiled=True)
    outgoing = memory_store[jnp.maximum(asked_for[:, 0], 0)]
    before, outgoing = lax.optimization_barrier((before, outgoing))
    returned = lax.all_to_all(outgoing, "seq", split_axis=0, concat_axis=0, tiled=True)
    shared = lax.psum(
      jnp.where(seq_index == owners - 1, memory_store[mem_dev - 1], jnp.zeros_like(memory_store[0])),
      "seq",
    )
    local_part = window_attention(
        queries, jnp.concatenate([before[0], keys]), jnp.concatenate([before[1], values]), first_row
    )
    mixing_row = jnp.repeat(jax.nn.sigmoid(gate_bias), HDIM)[None, :]
    block_count = tok_rows // QBLK
    block_order = jnp.arange(block_count, dtype=jnp.int32)
    attended = mixed_memory_attention(
        queries, returned, shared, local_part.reshape(tok_rows, features), mixing_row, block_order,
        owner_index, is_last.astype(jnp.int32), None, 0, block_count,
    )
    out_rows = tok_rows // groups
    gathered = lax.all_to_all(
        attended.reshape(groups, out_rows, features), "head", split_axis=0, concat_axis=0, tiled=True
    )
    head_index = lax.axis_index("head")
    own_rows = lax.dynamic_index_in_dim(
        attended.reshape(groups, out_rows, features), head_index, 0, keepdims=False
    )
    own_part = jnp.dot(own_rows, out_weight, preferred_element_type=jnp.float32).astype(jnp.bfloat16)
    return grouped_projection(
        own_part,
        gathered,
        full_weight.reshape(groups, features, full_weight.shape[1]),
        head_index.astype(jnp.int32).reshape(1),
    )


def solution(mesh):
    in_specs = (
        P("seq", "head"),
        P("seq", "head"),
        P("seq", "head"),
        P("seq", "head"),
        P("seq", "head"),
        P("seq", None),
        P("head"),
        P("head", None),
    )
    out_specs = P(("seq", "head"), None)
    return jax.shard_map(layer, mesh=mesh, in_specs=in_specs, out_specs=out_specs, check_vma=False)
```

```python
import math

import jax
import jax.numpy as jnp
from jax import lax
from jax.experimental import pallas as pl
from jax.experimental.pallas import tpu as pltpu
from jax.sharding import PartitionSpec as P


HDIM = 128
WINDOW = 1024
QBLK = 128
MROWS = 64
TOPM = 4


NEG_FILL = -1e30


def passed_along(value, axis, steps):
    count = lax.axis_size(axis)
    leading, last = (max(0, -steps), min(count, count - steps))
    return lax.ppermute(value, axis, [(source, source + steps) for source in range(leading, last)])


def masked_softmax(scores, allowed):
    row_max = jnp.max(jnp.where(allowed, scores, NEG_FILL), axis=-1, keepdims=True)
    weights = jnp.where(allowed, jnp.exp(scores - row_max), 0.0)
    return (weights / jnp.sum(weights, axis=-1, keepdims=True)).astype(jnp.bfloat16)


def window_attention(queries, ext_keys, ext_values, first_row):
    tok_rows, features = queries.shape
    heads_here = features // HDIM
    tile_rows = math.gcd(tok_rows, 512)
    key_span = tile_rows + WINDOW
    score_scale = 1.0 / math.sqrt(HDIM)

    def per_tile(step_index):
        row_start = step_index * tile_rows
        query_tile = lax.dynamic_slice_in_dim(queries, row_start, tile_rows, 0).reshape(
            tile_rows, heads_here, HDIM
        )
        key_tile = lax.dynamic_slice_in_dim(ext_keys, row_start, key_span, 0).reshape(
            key_span, heads_here, HDIM
        )
        value_tile = lax.dynamic_slice_in_dim(ext_values, row_start, key_span, 0).reshape(
            key_span, heads_here, HDIM
        )
        scores = (
            jnp.einsum("qhd,khd->hqk", query_tile, key_tile, preferred_element_type=jnp.float32)
            * score_scale
        )
        query_pos = first_row + row_start + jnp.arange(tile_rows, dtype=jnp.int32)
        key_pos = first_row + row_start - WINDOW + jnp.arange(key_span, dtype=jnp.int32)
        allowed = (
            (key_pos[None, :] <= query_pos[:, None])
            & (key_pos[None, :] > query_pos[:, None] - WINDOW)
            & (key_pos[None, :] >= 0)
        )
        attend_weights = masked_softmax(scores, allowed[None])
        return jnp.einsum(
            "hqk,khd->qhd", attend_weights, value_tile, preferred_element_type=jnp.float32
        )

    return lax.map(per_tile, jnp.arange(tok_rows // tile_rows, dtype=jnp.int32)).reshape(
        tok_rows, heads_here, HDIM
    )


def mixed_memory_attention(queries, returned, shared, local_part, mixing_row, slot_owner, slot_shared):
    tok_rows, features = queries.shape
    heads_here = features // HDIM
    score_scale = 1.0 / math.sqrt(HDIM)
    per_step = 4
    span = per_step * QBLK

    def kernel(owner_ref, flag_ref, q_ref, *refs):
        fetched = refs[: per_step * TOPM]
        sh_ref, loc_ref, mix_ref, out_ref = refs[per_step * TOPM :]
        for b in range(per_step):
            c = per_step * pl.program_id(0) + b
            rows = slice(b * QBLK, (b + 1) * QBLK)
            key_parts = []
            value_parts = []
            for j in range(TOPM):
                use_shared = flag_ref[c * TOPM + j] == 1
                block = fetched[b * TOPM + j]
                key_parts.append(jnp.where(use_shared, sh_ref[0], block[0, 0]))
                value_parts.append(jnp.where(use_shared, sh_ref[1], block[0, 1]))
            key_tile = jnp.concatenate(key_parts, axis=0)
            value_tile = jnp.concatenate(value_parts, axis=0)
            query_tile = q_ref[rows, :]
            for h in range(heads_here):
                cols = slice(h * HDIM, (h + 1) * HDIM)
                scores = (
                    lax.dot_general(
                        query_tile[:, cols],
                        key_tile[:, cols],
                        (((1,), (1,)), ((), ())),
                        preferred_element_type=jnp.float32,
                    )
                    * score_scale
                )
                row_max = jnp.max(scores, axis=-1, keepdims=True)
                weights = jnp.exp(scores - row_max)
                weights = (weights / jnp.sum(weights, axis=-1, keepdims=True)).astype(jnp.bfloat16)
                remote = jnp.dot(weights, value_tile[:, cols], preferred_element_type=jnp.float32)
                gate = mix_ref[:, cols]
                out_ref[rows, cols] = (
                    gate * remote + (1.0 - gate) * loc_ref[rows, cols]
                ).astype(jnp.bfloat16)

    def rows_spec():
        return pl.BlockSpec((span, features), lambda i, owner, flag: (i, 0))

    def fetched_spec(b, j):
        return pl.BlockSpec(
            (1, 2, MROWS, features),
            lambda i, owner, flag: (owner[(per_step * i + b) * TOPM + j], 0, 0, 0),
        )

    in_specs = (
        [rows_spec()]
        + [fetched_spec(b, j) for b in range(per_step) for j in range(TOPM)]
        + [
            pl.BlockSpec((2, MROWS, features), lambda i, owner, flag: (0, 0, 0)),
            rows_spec(),
            pl.BlockSpec((1, features), lambda i, owner, flag: (0, 0)),
        ]
    )
    grid_spec = pltpu.PrefetchScalarGridSpec(
        num_scalar_prefetch=2,
        grid=(tok_rows // span,),
        in_specs=in_specs,
        out_specs=rows_spec(),
    )
    return pl.pallas_call(
        kernel,
        grid_spec=grid_spec,
        out_shape=jax.ShapeDtypeStruct((tok_rows, features), jnp.bfloat16),
        compiler_params=pltpu.CompilerParams(dimension_semantics=("arbitrary",)),
    )(
        slot_owner,
        slot_shared,
        queries,
        *([returned] * (per_step * TOPM)),
        shared,
        local_part,
        mixing_row,
    )


def grouped_projection(own_part, gathered, weight, head_index):
    groups, rows, features = gathered.shape
    width = weight.shape[2]
    tile = math.gcd(width, 512)

    def kernel(head_ref, own_ref, *refs):
        parts = refs[: groups - 1]
        weights = refs[groups - 1 : 2 * (groups - 1)]
        o_ref = refs[-1]
        total = own_ref[...].astype(jnp.float32)
        for a_ref, w_ref in zip(parts, weights):
            part = jnp.dot(a_ref[0], w_ref[0], preferred_element_type=jnp.float32)
            total = total + part.astype(jnp.bfloat16).astype(jnp.float32)
        o_ref[...] = total.astype(jnp.bfloat16)

    def part_spec(k):
        return pl.BlockSpec((1, rows, features), lambda n, h: ((h[0] + k) % groups, 0, 0))

    def weight_spec(k):
        return pl.BlockSpec((1, features, tile), lambda n, h: ((h[0] + k) % groups, 0, n))

    others = range(1, groups)
    grid_spec = pltpu.PrefetchScalarGridSpec(
        num_scalar_prefetch=1,
        grid=(width // tile,),
        in_specs=[pl.BlockSpec((rows, tile), lambda n, h: (0, n))]
        + [part_spec(k) for k in others]
        + [weight_spec(k) for k in others],
        out_specs=pl.BlockSpec((rows, tile), lambda n, h: (0, n)),
    )
    return pl.pallas_call(
        kernel,
        grid_spec=grid_spec,
        out_shape=jax.ShapeDtypeStruct((rows, width), jnp.bfloat16),
        compiler_params=pltpu.CompilerParams(dimension_semantics=("arbitrary",)),
    )(head_index, own_part, *([gathered] * (groups - 1)), *([weight] * (groups - 1)))


def build_table(slot_index, offset, in_use, total_slots):
    matches = (jnp.arange(total_slots, dtype=jnp.int32)[:, None] == slot_index[None, :]) & in_use[
        None, :
    ]
    return jnp.sum(jnp.where(matches, offset[None, :] + 1, 0), axis=1) - 1


def layer(queries, keys, values, memory_keys, memory_values, block_ids, gate_bias, out_weight):
    tok_rows, features = queries.shape
    owners = lax.axis_size("seq")
    groups = lax.axis_size("head")
    seq_index = lax.axis_index("seq")
    first_row = seq_index * tok_rows
    full_weight = lax.all_gather(out_weight, "head", axis=0, tiled=True)
    request_count = block_ids.shape[0] * block_ids.shape[1]
    wanted = block_ids.reshape(request_count)
    mem_dev = memory_keys.shape[0] // MROWS
    last_block = owners * mem_dev - 1
    owner_index = wanted // mem_dev
    offset = wanted % mem_dev
    is_last = wanted == last_block
    memory_store = jnp.stack(
        (
            memory_keys.reshape(mem_dev, MROWS, features),
            memory_values.reshape(mem_dev, MROWS, features),
        ),
        axis=1,
    )
    slot_table = build_table(owner_index, offset, jnp.logical_not(is_last), owners).reshape(owners, 1)
    edge_rows = jnp.stack((keys, values))
    before = passed_along(edge_rows, "seq", 1)
    asked_for = lax.all_to_all(slot_table, "seq", split_axis=0, concat_axis=0, tiled=True)
    outgoing = memory_store[jnp.maximum(asked_for[:, 0], 0)]
    before, outgoing = lax.optimization_barrier((before, outgoing))
    returned = lax.all_to_all(outgoing, "seq", split_axis=0, concat_axis=0, tiled=True)
    shared = lax.psum(
      jnp.where(seq_index == owners - 1, memory_store[mem_dev - 1], jnp.zeros_like(memory_store[0])),
      "seq",
    )
    local_part = window_attention(
        queries, jnp.concatenate([before[0], keys]), jnp.concatenate([before[1], values]), first_row
    )
    mixing_row = jnp.repeat(jax.nn.sigmoid(gate_bias), HDIM)[None, :]
    attended = mixed_memory_attention(
        queries, returned, shared, local_part.reshape(tok_rows, features), mixing_row,
        owner_index, is_last.astype(jnp.int32),
    )
    out_rows = tok_rows // groups
    gathered = lax.all_to_all(
        attended.reshape(groups, out_rows, features), "head", split_axis=0, concat_axis=0, tiled=True
    )
    head_index = lax.axis_index("head")
    own_rows = lax.dynamic_index_in_dim(
        attended.reshape(groups, out_rows, features), head_index, 0, keepdims=False
    )
    own_part = jnp.dot(own_rows, out_weight, preferred_element_type=jnp.float32).astype(jnp.bfloat16)
    return grouped_projection(
        own_part,
        gathered,
        full_weight.reshape(groups, features, full_weight.shape[1]),
        head_index.astype(jnp.int32).reshape(1),
    )


def solution(mesh):
    in_specs = (
        P("seq", "head"),
        P("seq", "head"),
        P("seq", "head"),
        P("seq", "head"),
        P("seq", "head"),
        P("seq", None),
        P("head"),
        P("head", None),
    )
    out_specs = P(("seq", "head"), None)
    return jax.shard_map(layer, mesh=mesh, in_specs=in_specs, out_specs=out_specs, check_vma=False)
```
